256 devices in a mesh: group: 8 (over y, core), leaf: 32 (over z, x).
Axes of the slice: x: 4, y: 4, z: 8, core: 2. Of those that a mesh axis runs over, the one named last changes fastest.
Arguments:
- charge_input: float32 [32, 524288], P(None, ('group', 'leaf')), may hold values from -6 to 6
- points: float32 [3, 524288], P(None, ('group', 'leaf')), may hold values from 0 to 8192
- tree_order: int32 [256, 2048], P(('group', 'leaf')), may hold values from 0 to 2047, as said below
- cluster_basis: float32 [64, 524288], P(None, ('group', 'leaf')), may hold values from -0.75 to 0.75
- near_mask: int32 [6, 8192], P(None, ('group', 'leaf')), may hold values 0 or 1
- lower_mask: int32 [256, 7, 62], P(('group', 'leaf')), may hold values 0 or 1
- upper_mask: int32 [7, 504], replicated, may hold values 0 or 1
- transfer: float32 [9, 2, 64, 64], replicated, may hold values from -0.625 to 0.625
- coupling: float32 [10, 8, 64, 64], replicated, may hold values from -0.15625 to 0.15625
Outputs:
- potential: float32 [32, 524288], P(None, ('group', 'leaf'))
The draws below stay inside these ranges and needn't reach their ends.
Inputs may be any that keep to these rules, and one draw needn't show every extreme that they name: `tree_order`: each row is a permutation of 0 to 2047.
All inputs are finite; a program needn't handle non-finite values. No bound on the sum of `near_mask` or of `lower_mask` on one device may be relied on, other than what follows from the above.
Results may differ from the reference program's by a relative error of at most 0.0003.
Values sent between devices are 32-bit elements; how exact they have to be, the bound alone decides.
No kernel may reach another device: no remote copies, remote signals or barrier semaphores. Data moves between devices by JAX's collectives and lax.ppermute only.
A program may use at most 64 MiB of HBM per device.

```python
import jax
import jax.numpy as jnp
from jax import lax

K = 64
LS = 64
R = 32
LEAF_DEV = 32
LOG_LD = 5
NDEV = 256
NLEAF = 8192
PTS_DEV = 2048
NPTS = 524288
LOWER = 62
UPPER = 504
TRN = 9
CPL = 10


def order_table(key):
    key_list = jax.random.split(jax.random.fold_in(key, 11), NDEV)
    return jax.vmap(lambda single: jax.random.permutation(single, PTS_DEV))(key_list).astype(jnp.int32)


def draw_tree_order(key, part):
    return order_table(key)


def draw_points(key, part):
    positions = order_table(key)
    spread = jax.random.uniform(jax.random.fold_in(key, 12), (3, NDEV, PTS_DEV), jnp.float32)
    serial = jnp.arange(NDEV * PTS_DEV, dtype=jnp.int32).reshape(NDEV, PTS_DEV) // LS
    along_axis = serial.astype(jnp.float32) + spread[0]
    placed = jnp.stack([along_axis, spread[1], 0.5 * spread[2]], axis=0)
    devices = jnp.broadcast_to(jnp.arange(NDEV, dtype=jnp.int32)[:, None], (NDEV, PTS_DEV))
    shuffled = jnp.zeros((3, NDEV, PTS_DEV), jnp.float32).at[:, devices, positions].set(placed)
    return shuffled.reshape(3, NDEV * PTS_DEV)


def touch_ends(entries, key, smallest, high):
    spot = [jax.random.randint(jax.random.fold_in(key, axis), (), 0, length) for axis, length in enumerate(entries.shape)]
    main_axis = entries.shape.index(max(entries.shape))
    beside = spot[:main_axis] + [(spot[main_axis] + 1) % entries.shape[main_axis]] + spot[main_axis + 1:]
    return entries.at[tuple(spot)].set(smallest).at[tuple(beside)].set(high)


def shard_levels(own_key, shape, cuts, least, largest):
    gain, own = 1.0, jax.random.fold_in(own_key, 6)
    for dim, parts in cuts:
        draws = jnp.exp(jax.random.uniform(jax.random.fold_in(own, dim), (parts,), jnp.float32, least / len(cuts), largest / len(cuts)))
        gain = gain * jnp.repeat(draws, shape[dim] // parts).reshape([-1 if axis == dim else 1 for axis in range(len(shape))])
    return gain


def normal_values(stream_key, dims, scale, most, cuts=(), kind=jnp.bfloat16):
    entries = scale * jax.random.normal(stream_key, dims, jnp.float32)
    if cuts:
        entries = entries * shard_levels(stream_key, dims, cuts, -0.22, 0.18)
    return jnp.clip(entries, -most, most).astype(kind)


def setup_inputs(seed: int = 0) -> dict:
    seeds = jax.random.split(jax.random.key(seed), 10)
    return {
        "charge_input": normal_values(seeds[0], (R, NPTS), 1.0, 6.0, ((1, 256),), jnp.float32),
        "points": draw_points(jax.random.fold_in(seeds[9], 71), 0),
        "tree_order": draw_tree_order(jax.random.fold_in(seeds[9], 71), 0),
        "cluster_basis": normal_values(seeds[3], (K, NPTS), LS ** -0.5, 0.75, ((1, 256),), jnp.float32),
        "near_mask": touch_ends((jax.random.randint(seeds[4], (6, NLEAF), 0, 4) < 3).astype(jnp.int32), jax.random.fold_in(seeds[4], 1), 0, 1),
        "lower_mask": touch_ends((jax.random.randint(seeds[5], (NDEV, 7, LOWER), 0, 4) < 3).astype(jnp.int32), jax.random.fold_in(seeds[5], 1), 0, 1),
        "upper_mask": touch_ends((jax.random.randint(seeds[6], (7, UPPER), 0, 4) < 3).astype(jnp.int32), jax.random.fold_in(seeds[6], 1), 0, 1),
        "transfer": normal_values(seeds[7], (TRN, 2, K, K), (K * 1414 // 1000) ** -0.5, 0.625, (), jnp.float32),
        "coupling": normal_values(seeds[8], (CPL, 8, K, K), (20 * K) ** -0.5, 0.15625, (), jnp.float32),
    }


KERNEL_SCALE = 0.0625
SOFTENING = 0.01
OFFSETS = (-7, -6, -5, -4, 4, 5, 6, 7)
highest = lax.Precision.HIGHEST

def near_field(charge_window, point_window, near_mask):
    leaves = near_mask.shape[1]
    right_sides = charge_window.shape[0]
    charge_grid = charge_window.reshape(right_sides, leaves + 6, LS).transpose(0, 2, 1)
    point_grid = point_window.reshape(3, leaves + 6, LS).transpose(0, 2, 1)
    target = point_grid[:, :, 3:3 + leaves]
    summed = jnp.zeros((right_sides, LS, leaves), jnp.float32)
    for position, offset in enumerate((-3, -2, -1, 0, 1, 2, 3)):
        source = point_grid[:, :, 3 + offset:3 + offset + leaves]
        separation = target[:, :, None, :] - source[:, None, :, :]
        kernel = KERNEL_SCALE * lax.rsqrt(lax.optimization_barrier(jnp.sum(separation * separation, axis=0)) + SOFTENING)
        product = jnp.einsum('abl,rbl->ral', kernel, charge_grid[:, :, 3 + offset:3 + offset + leaves], precision=highest)
        if offset != 0:
            mask_row = position if offset < 0 else position - 1
            product = product * near_mask[mask_row].astype(jnp.float32)[None, None, :]
        summed = summed + product
    return summed.transpose(0, 2, 1).reshape(right_sides, leaves * LS)

def slot_weights(live_slots, is_even):
    is_odd = 1.0 - is_even
    return (live_slots[6] * is_odd, live_slots[0], live_slots[1], live_slots[2], live_slots[3], live_slots[4], live_slots[5], live_slots[6] * is_even)

def couple_window(padded, coupling_table, weights, reach_cells):
    clusters = padded.shape[1] - 2 * reach_cells
    extended = jnp.pad(padded, ((0, 0), (1, 1), (0, 0)))
    summed = None
    for position, offset in enumerate(OFFSETS):
        first_col = reach_cells + 1 + offset
        source = extended[:, first_col:first_col + clusters] * weights[position][None, :, None]
        product = jnp.einsum('ij,jnr->inr', coupling_table[position], source, precision=highest)
        summed = product if summed is None else summed + product
    return summed

def raise_level(matrix, coeffs):
    return jnp.einsum('jk,jnr->knr', matrix, coeffs, precision=highest)

def lower_level(matrix, coeffs):
    return jnp.einsum('kj,jnr->knr', matrix, coeffs, precision=highest)

def alternate_children(first_child, second_child):
    stacked = jnp.stack([first_child, second_child], axis=2)
    return stacked.reshape(first_child.shape[0], 2 * first_child.shape[1], first_child.shape[2])

def reference(charge_input, points, tree_order, cluster_basis, near_mask, lower_mask, upper_mask, transfer, coupling):
    shifts = (jnp.arange(NDEV, dtype=jnp.int32) * PTS_DEV)[:, None]
    tree_positions = (tree_order + shifts).reshape(NPTS)
    charges = charge_input[:, tree_positions]
    coords = points[:, tree_positions]
    charge_padded = jnp.pad(charges, ((0, 0), (3 * LS, 3 * LS)))
    point_padded = jnp.pad(coords, ((0, 0), (3 * LS, 3 * LS)))

    def one_device(device_index):
        first_col = device_index * PTS_DEV
        charge_window = lax.dynamic_slice_in_dim(charge_padded, first_col, PTS_DEV + 6 * LS, 1)
        point_window = lax.dynamic_slice_in_dim(point_padded, first_col, PTS_DEV + 6 * LS, 1)
        mask_window = lax.dynamic_slice_in_dim(near_mask, device_index * LEAF_DEV, LEAF_DEV, 1)
        return near_field(charge_window, point_window, mask_window)
    near_blocks = lax.map(one_device, jnp.arange(NDEV, dtype=jnp.int32))
    near_part = near_blocks.transpose(1, 0, 2).reshape(R, NPTS)
    leaf_basis = cluster_basis.reshape(K, NLEAF, LS)
    upward = [jnp.einsum('kla,rla->klr', leaf_basis, charges.reshape(R, NLEAF, LS), precision=highest)]
    for tree_level in range(CPL - 1):
        coeffs = upward[-1]
        upward.append(raise_level(transfer[tree_level, 0], coeffs[:, 0::2]) + raise_level(transfer[tree_level, 1], coeffs[:, 1::2]))
    coupled = []
    for tree_level in range(CPL):
        coeffs = upward[tree_level]
        clusters = coeffs.shape[1]
        if tree_level < LOG_LD:
            per_device = LEAF_DEV // 2 ** tree_level
            first_row = 2 * LEAF_DEV - 2 * per_device
            live_slots = lower_mask[:, :, first_row:first_row + per_device].transpose(1, 0, 2).reshape(7, clusters)
        else:
            per_group = NDEV // 2 ** (tree_level - LOG_LD)
            first_row = 2 * NDEV - 2 * per_group
            live_slots = upper_mask[:, first_row:first_row + per_group]
        is_even = (jnp.arange(clusters) % 2 == 0).astype(jnp.float32)
        padded = jnp.pad(coeffs, ((0, 0), (6, 6), (0, 0)))
        weights = slot_weights(live_slots.astype(jnp.float32), is_even)
        coupled.append(couple_window(padded, coupling[tree_level], weights, 6))
    far_field = coupled[CPL - 1]
    for tree_level in range(CPL - 2, -1, -1):
        far_field = coupled[tree_level] + alternate_children(lower_level(transfer[tree_level, 0], far_field), lower_level(transfer[tree_level, 1], far_field))
    far_part = jnp.einsum('klr,kla->rla', far_field, leaf_basis, precision=highest).reshape(R, NPTS)
    potential_tree = near_part + far_part
    return jnp.zeros((R, NPTS), jnp.float32).at[:, tree_positions].set(potential_tree)
```

```python
import jax
import jax.numpy as jnp
from jax import lax
from jax.sharding import PartitionSpec as P

K = 64
LS = 64
LEAF_DEV = 32
LOG_LD = 5


KERNEL_SCALE = 0.0625
SOFTENING = 0.01
OFFSETS = (-7, -6, -5, -4, 4, 5, 6, 7)
highest = lax.Precision.HIGHEST


def from_behind(shard, axis, by):
    peers = lax.axis_size(axis)
    pairs = [(i, i + by) for i in range(peers) if 0 <= i + by < peers]
    return lax.ppermute(shard, axis, pairs)


def extended_2(shard, sides, width):
    for axis, dim in sides:
        peers, length = (lax.axis_size(axis), shard.shape[dim])
        up = [(i, (i + 1) % peers) for i in range(peers - 1)]
        down = [(j, i) for i, j in up]
        last = lax.slice_in_dim(shard, length - width, length, axis=dim)
        first = lax.slice_in_dim(shard, 0, width, axis=dim)
        before = lax.ppermute(last, axis, up)
        after = lax.ppermute(first, axis, down)
        shard = jnp.concatenate([before, shard, after], axis=dim)
    return shard


def from_partner(block, axis, stride):
    count = lax.axis_size(axis)
    route = []
    for low in range(count):
        high = low | 1 << stride
        if high != low and high < count:
            route += [(low, high), (high, low)]
    return lax.ppermute(block, axis, route)


def near_field(charge_window, point_window, near_mask):
    leaves = near_mask.shape[1]
    right_sides = charge_window.shape[0]
    charge_grid = charge_window.reshape(right_sides, leaves + 6, LS).transpose(0, 2, 1)
    point_grid = point_window.reshape(3, leaves + 6, LS).transpose(0, 2, 1)
    target = point_grid[:, :, 3 : 3 + leaves]
    summed = jnp.zeros((right_sides, LS, leaves), jnp.float32)
    for position, offset in enumerate((-3, -2, -1, 0, 1, 2, 3)):
        source = point_grid[:, :, 3 + offset : 3 + offset + leaves]
        separation = target[:, :, None, :] - source[:, None, :, :]
        kernel = KERNEL_SCALE * lax.rsqrt(jnp.sum(separation * separation, axis=0) + SOFTENING)
        product = jnp.einsum(
            "abl,rbl->ral",
            kernel,
            charge_grid[:, :, 3 + offset : 3 + offset + leaves],
            precision=highest,
        )
        if offset != 0:
            mask_row = position if offset < 0 else position - 1
            product = product * near_mask[mask_row].astype(jnp.float32)[None, None, :]
        summed = summed + product
    return summed.transpose(0, 2, 1).reshape(right_sides, leaves * LS)


def slot_weights(live_slots, is_even):
    is_odd = 1.0 - is_even
    return (
        live_slots[6] * is_odd,
        live_slots[0],
        live_slots[1],
        live_slots[2],
        live_slots[3],
        live_slots[4],
        live_slots[5],
        live_slots[6] * is_even,
    )


def couple_window(padded, coupling_table, weights, reach_cells):
    clusters = padded.shape[1] - 2 * reach_cells
    extended = jnp.pad(padded, ((0, 0), (1, 1), (0, 0)))
    summed = None
    for position, offset in enumerate(OFFSETS):
        first_col = reach_cells + 1 + offset
        source = extended[:, first_col : first_col + clusters] * weights[position][None, :, None]
        product = jnp.einsum("ij,jnr->inr", coupling_table[position], source, precision=highest)
        summed = product if summed is None else summed + product
    return summed


def raise_level(matrix, coeffs):
    return jnp.einsum("jk,jnr->knr", matrix, coeffs, precision=highest)


def lower_level(matrix, coeffs):
    return jnp.einsum("kj,jnr->knr", matrix, coeffs, precision=highest)


def alternate_children(first_child, second_child):
    stacked = jnp.stack([first_child, second_child], axis=2)
    return stacked.reshape(first_child.shape[0], 2 * first_child.shape[1], first_child.shape[2])


AXES = ("group", "leaf")


def exchange(shard, by):
    return from_behind(shard, AXES, by)


def upper_far_field(top, device_index, device_count, upper_mask, transfer, coupling):
    log_dev = device_count.bit_length() - 1
    levels = [lax.all_gather(top, AXES, axis=0, tiled=False)]
    for height in range(log_dev - 4):
        coeffs = levels[-1]
        table = transfer[LOG_LD + height]
        levels.append(
            jnp.einsum("jk,njr->nkr", table[0], coeffs[0::2], precision=highest)
            + jnp.einsum("jk,njr->nkr", table[1], coeffs[1::2], precision=highest)
        )
    reach = max(OFFSETS)
    picks = [reach + offset for offset in OFFSETS]
    windows = []
    for height in range(log_dev - 3):
        coeffs = levels[height]
        clusters = coeffs.shape[0]
        cluster = device_index // 2**height
        padded = jnp.pad(coeffs, ((reach, reach), (0, 0), (0, 0)))
        window = lax.dynamic_slice_in_dim(padded, cluster, 2 * reach + 1, axis=0)[jnp.array(picks)]
        mask_row = 2 * device_count - 2 * clusters + cluster
        live_slots = lax.dynamic_index_in_dim(upper_mask, mask_row, 1, keepdims=False).astype(
            jnp.float32
        )
        weights = jnp.stack(slot_weights(live_slots, (cluster % 2 == 0).astype(jnp.float32)))
        windows.append(window * weights[:, None, None])
    stacked = jnp.stack(windows)
    coupled = jnp.einsum(
        "hpij,hpjr->hir", coupling[LOG_LD : LOG_LD + log_dev - 3], stacked, precision=highest
    )
    far_field = coupled[-1]
    for height in range(log_dev - 5, -1, -1):
        side_bit = device_index // 2**height % 2
        far_field = coupled[height] + jnp.dot(
            transfer[LOG_LD + height][side_bit], far_field, precision=highest
        )
    return far_field


def local(
    charge_input,
    points,
    tree_order,
    cluster_basis,
    near_mask,
    lower_mask,
    upper_mask,
    transfer,
    coupling,
):
    device_count = lax.axis_size(AXES)
    device_index = lax.axis_index(AXES)
    tree_positions = tree_order[0]
    charges = charge_input[:, tree_positions]
    coords = points[:, tree_positions]
    right_sides = charges.shape[0]
    stacked = jnp.concatenate([charges, coords], axis=0)
    rows, width = stacked.shape[0], 3 * LS
    leaf_basis = cluster_basis.reshape(K, LEAF_DEV, LS)
    upward = [
        jnp.einsum(
            "kla,rla->klr",
            leaf_basis,
            charges.reshape(right_sides, LEAF_DEV, LS),
            precision=highest,
        )
    ]
    for tree_level in range(LOG_LD):
        coeffs = upward[-1]
        upward.append(
            raise_level(transfer[tree_level, 0], coeffs[:, 0::2])
            + raise_level(transfer[tree_level, 1], coeffs[:, 1::2])
        )
    left_parts = [[], [], [], []]
    right_parts = [[], [], [], []]
    for tree_level in range(LOG_LD):
        coeffs = upward[tree_level]
        clusters = coeffs.shape[1]
        for distance in range(1, -(-6 // clusters) + 1):
            left_parts[distance].append(coeffs[:, max(0, distance * clusters - 6) :])
            right_parts[distance].append(coeffs[:, : min(clusters, 6 - (distance - 1) * clusters)])
    from_left = [None, None, None, None]
    from_right = [None, None, None, None]
    halo_size = rows * width
    for distance in range(1, 4):
        packed_left = jnp.concatenate(left_parts[distance], axis=1)
        packed_right = jnp.concatenate(right_parts[distance], axis=1)
        if distance == 1:
            flat_left = jnp.concatenate(
                [stacked[:, -width:].reshape(-1), packed_left.reshape(-1)]
            )
            flat_right = jnp.concatenate(
                [stacked[:, :width].reshape(-1), packed_right.reshape(-1)]
            )
            got_left = exchange(flat_left, 1)
            got_right = exchange(flat_right, -1)
            halo_before = got_left[:halo_size].reshape(rows, width)
            halo_after = got_right[:halo_size].reshape(rows, width)
            from_left[1] = got_left[halo_size:].reshape(packed_left.shape)
            from_right[1] = got_right[halo_size:].reshape(packed_right.shape)
        else:
            from_left[distance] = exchange(packed_left, distance)
            from_right[distance] = exchange(packed_right, -distance)
    widened = jnp.concatenate([halo_before, stacked, halo_after], axis=1)
    near_part = near_field(widened[:right_sides], widened[right_sides:], near_mask)
    cursors_left = [0, 0, 0, 0]
    cursors_right = [0, 0, 0, 0]
    coupled_local = []
    for tree_level in range(LOG_LD):
        coeffs = upward[tree_level]
        clusters = coeffs.shape[1]
        reach_devices = -(-6 // clusters)
        before = []
        beyond = []
        for distance in range(reach_devices, 0, -1):
            piece_width = clusters - max(0, distance * clusters - 6)
            before.append(
                from_left[distance][
                    :, cursors_left[distance] : cursors_left[distance] + piece_width
                ]
            )
            cursors_left[distance] += piece_width
        for distance in range(1, reach_devices + 1):
            piece_width = min(clusters, 6 - (distance - 1) * clusters)
            beyond.append(
                from_right[distance][
                    :, cursors_right[distance] : cursors_right[distance] + piece_width
                ]
            )
            cursors_right[distance] += piece_width
        padded = jnp.concatenate(before + [coeffs] + beyond, axis=1)
        first_row = 2 * LEAF_DEV - 2 * clusters
        live_slots = lower_mask[0][:, first_row : first_row + clusters].astype(jnp.float32)
        is_even = (jnp.arange(clusters) % 2 == 0).astype(jnp.float32)
        coupled_local.append(
            couple_window(padded, coupling[tree_level], slot_weights(live_slots, is_even), 6)
        )
    far_field = upper_far_field(
        upward[LOG_LD][:, 0], device_index, device_count, upper_mask, transfer, coupling
    )
    far_field = far_field[:, None, :]
    for tree_level in range(LOG_LD - 1, -1, -1):
        far_field = coupled_local[tree_level] + alternate_children(
            lower_level(transfer[tree_level, 0], far_field),
            lower_level(transfer[tree_level, 1], far_field),
        )
    far_part = jnp.einsum("klr,kla->rla", far_field, leaf_basis, precision=highest).reshape(
        right_sides, LEAF_DEV * LS
    )
    potential_tree = near_part + far_part
    return jnp.zeros_like(potential_tree).at[:, tree_positions].set(potential_tree)


def solution(mesh):
    placed = (
        P(None, ("group", "leaf")),
        P(None, ("group", "leaf")),
        P(("group", "leaf"), None),
        P(None, ("group", "leaf")),
        P(None, ("group", "leaf")),
        P(("group", "leaf"), None, None),
        P(),
        P(),
        P(),
    )
    return jax.shard_map(
        local, mesh=mesh, in_specs=placed, out_specs=P(None, ("group", "leaf")), check_vma=False
    )
```

```python
import jax
import jax.numpy as jnp
from jax import lax
from jax.sharding import PartitionSpec as P

K = 64
LS = 64
LEAF_DEV = 32
LOG_LD = 5


KERNEL_SCALE = 0.0625
SOFTENING = 0.01
OFFSETS = (-7, -6, -5, -4, 4, 5, 6, 7)
highest = lax.Precision.HIGHEST


def from_behind(shard, axis, by):
    peers = lax.axis_size(axis)
    pairs = [(i, i + by) for i in range(peers) if 0 <= i + by < peers]
    return lax.ppermute(shard, axis, pairs)


def extended_2(shard, sides, width):
    for axis, dim in sides:
        peers, length = (lax.axis_size(axis), shard.shape[dim])
        up = [(i, (i + 1) % peers) for i in range(peers - 1)]
        down = [(j, i) for i, j in up]
        last = lax.slice_in_dim(shard, length - width, length, axis=dim)
        first = lax.slice_in_dim(shard, 0, width, axis=dim)
        before = lax.ppermute(last, axis, up)
        after = lax.ppermute(first, axis, down)
        shard = jnp.concatenate([before, shard, after], axis=dim)
    return shard


def from_partner(block, axis, stride):
    count = lax.axis_size(axis)
    route = []
    for low in range(count):
        high = low | 1 << stride
        if high != low and high < count:
            route += [(low, high), (high, low)]
    return lax.ppermute(block, axis, route)


def near_field(charge_window, point_window, near_mask):
    leaves = near_mask.shape[1]
    right_sides = charge_window.shape[0]
    charge_grid = charge_window.reshape(right_sides, leaves + 6, LS).transpose(0, 2, 1)
    point_grid = point_window.reshape(3, leaves + 6, LS).transpose(0, 2, 1)
    target = point_grid[:, :, 3 : 3 + leaves]
    offsets = (-3, -2, -1, 0, 1, 2, 3)
    sources = jnp.stack([point_grid[:, :, 3 + o : 3 + o + leaves] for o in offsets], axis=1)
    separation = target[:, None, :, None, :] - sources[:, :, None, :, :]
    ones = jnp.ones((1, leaves), jnp.float32)
    masks = near_mask.astype(jnp.float32)
    weight = jnp.concatenate([masks[:3], ones, masks[3:]], axis=0)
    kernel = KERNEL_SCALE * lax.rsqrt(jnp.sum(separation * separation, axis=0) + SOFTENING)
    kernel = kernel * weight[:, None, None, :]
    charges = jnp.stack([charge_grid[:, :, 3 + o : 3 + o + leaves] for o in offsets], axis=1)
    summed = jnp.einsum("oabl,robl->ral", kernel, charges, precision=highest)
    return summed.transpose(0, 2, 1).reshape(right_sides, leaves * LS)


def slot_weights(live_slots, is_even):
    is_odd = 1.0 - is_even
    return (
        live_slots[6] * is_odd,
        live_slots[0],
        live_slots[1],
        live_slots[2],
        live_slots[3],
        live_slots[4],
        live_slots[5],
        live_slots[6] * is_even,
    )


def couple_window(padded, coupling_table, weights, reach_cells):
    clusters = padded.shape[1] - 2 * reach_cells
    extended = jnp.pad(padded, ((0, 0), (1, 1), (0, 0)))
    sources = []
    for position, offset in enumerate(OFFSETS):
        first_col = reach_cells + 1 + offset
        sources.append(extended[:, first_col : first_col + clusters] * weights[position][None, :, None])
    stacked = jnp.stack(sources, axis=0)
    return jnp.einsum("pij,pjnr->inr", coupling_table, stacked, precision=highest)


def raise_pairs(table, coeffs):
    pairs = coeffs.reshape(coeffs.shape[0], coeffs.shape[1] // 2, 2, coeffs.shape[2])
    return jnp.einsum("pjk,jcpr->kcr", table, pairs, precision=highest)


def lower_pairs(table, coeffs):
    children = jnp.einsum("pkj,jnr->knpr", table, coeffs, precision=highest)
    return children.reshape(coeffs.shape[0], 2 * coeffs.shape[1], coeffs.shape[2])


def raise_level(matrix, coeffs):
    return jnp.einsum("jk,jnr->knr", matrix, coeffs, precision=highest)


def lower_level(matrix, coeffs):
    return jnp.einsum("kj,jnr->knr", matrix, coeffs, precision=highest)


def alternate_children(first_child, second_child):
    stacked = jnp.stack([first_child, second_child], axis=2)
    return stacked.reshape(first_child.shape[0], 2 * first_child.shape[1], first_child.shape[2])


AXES = ("group", "leaf")


def exchange(shard, by):
    return from_behind(shard, AXES, by)


def upper_far_field(top, device_index, device_count, upper_mask, transfer, coupling):
    log_dev = device_count.bit_length() - 1
    levels = [lax.all_gather(top, AXES, axis=0, tiled=False)]
    for height in range(log_dev - 4):
        coeffs = levels[-1]
        pairs = coeffs.reshape(coeffs.shape[0] // 2, 2, coeffs.shape[1], coeffs.shape[2])
        levels.append(
            jnp.einsum("pjk,cpjr->ckr", transfer[LOG_LD + height], pairs, precision=highest)
        )
    reach = max(OFFSETS)
    picks = [reach + offset for offset in OFFSETS]
    windows = []
    for height in range(log_dev - 3):
        coeffs = levels[height]
        clusters = coeffs.shape[0]
        cluster = device_index // 2**height
        padded = jnp.pad(coeffs, ((reach, reach), (0, 0), (0, 0)))
        window = lax.dynamic_slice_in_dim(padded, cluster, 2 * reach + 1, axis=0)
        window = jnp.concatenate([window[: picks[3] + 1], window[picks[4] :]], axis=0)
        mask_row = 2 * device_count - 2 * clusters + cluster
        live_slots = lax.dynamic_index_in_dim(upper_mask, mask_row, 1, keepdims=False).astype(
            jnp.float32
        )
        weights = jnp.stack(slot_weights(live_slots, (cluster % 2 == 0).astype(jnp.float32)))
        windows.append(window * weights[:, None, None])
    stacked = jnp.stack(windows)
    coupled = jnp.einsum(
        "hpij,hpjr->hir", coupling[LOG_LD : LOG_LD + log_dev - 3], stacked, precision=highest
    )
    far_field = coupled[-1]
    for height in range(log_dev - 5, -1, -1):
        side_bit = device_index // 2**height % 2
        far_field = coupled[height] + jnp.dot(
            transfer[LOG_LD + height][side_bit], far_field, precision=highest
        )
    return far_field


def local(
    charge_input,
    points,
    tree_order,
    cluster_basis,
    near_mask,
    lower_mask,
    upper_mask,
    transfer,
    coupling,
):
    device_count = lax.axis_size(AXES)
    device_index = lax.axis_index(AXES)
    tree_positions = tree_order[0]
    right_sides = charge_input.shape[0]
    stacked = jnp.concatenate([charge_input, points], axis=0)[:, tree_positions]
    charges = stacked[:right_sides]
    rows, width = stacked.shape[0], 3 * LS
    leaf_basis = cluster_basis.reshape(K, LEAF_DEV, LS)
    upward = [
        jnp.einsum(
            "kla,rla->klr",
            leaf_basis,
            charges.reshape(right_sides, LEAF_DEV, LS),
            precision=highest,
        )
    ]
    for tree_level in range(LOG_LD):
        coeffs = upward[-1]
        upward.append(raise_pairs(transfer[tree_level], coeffs))
    left_parts = [[], [], [], []]
    right_parts = [[], [], [], []]
    for tree_level in range(LOG_LD):
        coeffs = upward[tree_level]
        clusters = coeffs.shape[1]
        for distance in range(1, -(-6 // clusters) + 1):
            left_parts[distance].append(coeffs[:, max(0, distance * clusters - 6) :])
            right_parts[distance].append(coeffs[:, : min(clusters, 6 - (distance - 1) * clusters)])
    from_left = [None, None, None, None]
    from_right = [None, None, None, None]
    halo_size = rows * width
    for distance in range(1, 4):
        packed_left = jnp.concatenate(left_parts[distance], axis=1)
        packed_right = jnp.concatenate(right_parts[distance], axis=1)
        if distance == 1:
            flat_left = jnp.concatenate(
                [stacked[:, -width:].reshape(-1), packed_left.reshape(-1)]
            )
            flat_right = jnp.concatenate(
                [stacked[:, :width].reshape(-1), packed_right.reshape(-1)]
            )
            got_left = exchange(flat_left, 1)
            got_right = exchange(flat_right, -1)
            halo_before = got_left[:halo_size].reshape(rows, width)
            halo_after = got_right[:halo_size].reshape(rows, width)
            from_left[1] = got_left[halo_size:].reshape(packed_left.shape)
            from_right[1] = got_right[halo_size:].reshape(packed_right.shape)
        else:
            from_left[distance] = exchange(packed_left, distance)
            from_right[distance] = exchange(packed_right, -distance)
    widened = jnp.concatenate([halo_before, stacked, halo_after], axis=1)
    near_part = near_field(widened[:right_sides], widened[right_sides:], near_mask)
    cursors_left = [0, 0, 0, 0]
    cursors_right = [0, 0, 0, 0]
    coupled_local = []
    for tree_level in range(LOG_LD):
        coeffs = upward[tree_level]
        clusters = coeffs.shape[1]
        reach_devices = -(-6 // clusters)
        before = []
        beyond = []
        for distance in range(reach_devices, 0, -1):
            piece_width = clusters - max(0, distance * clusters - 6)
            before.append(
                from_left[distance][
                    :, cursors_left[distance] : cursors_left[distance] + piece_width
                ]
            )
            cursors_left[distance] += piece_width
        for distance in range(1, reach_devices + 1):
            piece_width = min(clusters, 6 - (distance - 1) * clusters)
            beyond.append(
                from_right[distance][
                    :, cursors_right[distance] : cursors_right[distance] + piece_width
                ]
            )
            cursors_right[distance] += piece_width
        padded = jnp.concatenate(before + [coeffs] + beyond, axis=1)
        first_row = 2 * LEAF_DEV - 2 * clusters
        live_slots = lower_mask[0][:, first_row : first_row + clusters].astype(jnp.float32)
        is_even = (jnp.arange(clusters) % 2 == 0).astype(jnp.float32)
        coupled_local.append(
            couple_window(padded, coupling[tree_level], slot_weights(live_slots, is_even), 6)
        )
    far_field = upper_far_field(
        upward[LOG_LD][:, 0], device_index, device_count, upper_mask, transfer, coupling
    )
    far_field = far_field[:, None, :]
    for tree_level in range(LOG_LD - 1, -1, -1):
        far_field = coupled_local[tree_level] + lower_pairs(transfer[tree_level], far_field)
    far_part = jnp.einsum("klr,kla->rla", far_field, leaf_basis, precision=highest).reshape(
        right_sides, LEAF_DEV * LS
    )
    potential_tree = near_part + far_part
    return jnp.zeros_like(potential_tree).at[:, tree_positions].set(potential_tree)


def solution(mesh):
    placed = (
        P(None, ("group", "leaf")),
        P(None, ("group", "leaf")),
        P(("group", "leaf"), None),
        P(None, ("group", "leaf")),
        P(None, ("group", "leaf")),
        P(("group", "leaf"), None, None),
        P(),
        P(),
        P(),
    )
    return jax.shard_map(
        local, mesh=mesh, in_specs=placed, out_specs=P(None, ("group", "leaf")), check_vma=False
    )
```

```python
import jax
import jax.numpy as jnp
from jax import lax
from jax.sharding import PartitionSpec as P

K = 64
LS = 64
LEAF_DEV = 32
LOG_LD = 5


KERNEL_SCALE = 0.0625
SOFTENING = 0.01
OFFSETS = (-7, -6, -5, -4, 4, 5, 6, 7)
highest = lax.Precision.HIGHEST


def from_behind(shard, axis, by):
    peers = lax.axis_size(axis)
    pairs = [(i, i + by) for i in range(peers) if 0 <= i + by < peers]
    return lax.ppermute(shard, axis, pairs)


def extended_2(shard, sides, width):
    for axis, dim in sides:
        peers, length = (lax.axis_size(axis), shard.shape[dim])
        up = [(i, (i + 1) % peers) for i in range(peers - 1)]
        down = [(j, i) for i, j in up]
        last = lax.slice_in_dim(shard, length - width, length, axis=dim)
        first = lax.slice_in_dim(shard, 0, width, axis=dim)
        before = lax.ppermute(last, axis, up)
        after = lax.ppermute(first, axis, down)
        shard = jnp.concatenate([before, shard, after], axis=dim)
    return shard


def from_partner(block, axis, stride):
    count = lax.axis_size(axis)
    route = []
    for low in range(count):
        high = low | 1 << stride
        if high != low and high < count:
            route += [(low, high), (high, low)]
    return lax.ppermute(block, axis, route)


def near_field(charge_window, point_window, near_mask):
    leaves = near_mask.shape[1]
    right_sides = charge_window.shape[0]
    charge_grid = charge_window.reshape(right_sides, leaves + 6, LS).transpose(0, 2, 1)
    point_grid = point_window.reshape(3, leaves + 6, LS).transpose(0, 2, 1)
    target = point_grid[:, :, 3 : 3 + leaves]
    offsets = (-3, -2, -1, 0, 1, 2, 3)
    sources = jnp.stack([point_grid[:, :, 3 + o : 3 + o + leaves] for o in offsets], axis=1)
    separation = target[:, None, :, None, :] - sources[:, :, None, :, :]
    ones = jnp.ones((1, leaves), jnp.float32)
    masks = near_mask.astype(jnp.float32)
    weight = jnp.concatenate([masks[:3], ones, masks[3:]], axis=0)
    kernel = KERNEL_SCALE * lax.rsqrt(jnp.sum(separation * separation, axis=0) + SOFTENING)
    kernel = kernel * weight[:, None, None, :]
    charges = jnp.stack([charge_grid[:, :, 3 + o : 3 + o + leaves] for o in offsets], axis=1)
    summed = jnp.einsum("oabl,robl->ral", kernel, charges, precision=highest)
    return summed.transpose(0, 2, 1).reshape(right_sides, leaves * LS)


def slot_weights(live_slots, is_even):
    is_odd = 1.0 - is_even
    return (
        live_slots[6] * is_odd,
        live_slots[0],
        live_slots[1],
        live_slots[2],
        live_slots[3],
        live_slots[4],
        live_slots[5],
        live_slots[6] * is_even,
    )


def couple_window(padded, coupling_table, weights, reach_cells):
    clusters = padded.shape[1] - 2 * reach_cells
    extended = jnp.pad(padded, ((0, 0), (1, 1), (0, 0)))
    products = jnp.einsum("pij,jmr->pimr", coupling_table, extended, precision=highest)
    summed = None
    for position, offset in enumerate(OFFSETS):
        first_col = reach_cells + 1 + offset
        term = products[position, :, first_col : first_col + clusters] * weights[position][None, :, None]
        summed = term if summed is None else summed + term
    return summed


def raise_pairs(table, coeffs):
    pairs = coeffs.reshape(coeffs.shape[0], coeffs.shape[1] // 2, 2, coeffs.shape[2])
    return jnp.einsum("pjk,jcpr->kcr", table, pairs, precision=highest)


def lower_pairs(table, coeffs):
    children = jnp.einsum("pkj,jnr->knpr", table, coeffs, precision=highest)
    return children.reshape(coeffs.shape[0], 2 * coeffs.shape[1], coeffs.shape[2])


def raise_level(matrix, coeffs):
    return jnp.einsum("jk,jnr->knr", matrix, coeffs, precision=highest)


def lower_level(matrix, coeffs):
    return jnp.einsum("kj,jnr->knr", matrix, coeffs, precision=highest)


def alternate_children(first_child, second_child):
    stacked = jnp.stack([first_child, second_child], axis=2)
    return stacked.reshape(first_child.shape[0], 2 * first_child.shape[1], first_child.shape[2])


AXES = ("group", "leaf")


def exchange(shard, by):
    return from_behind(shard, AXES, by)


def upper_far_field(top, device_index, device_count, upper_mask, transfer, coupling):
    log_dev = device_count.bit_length() - 1
    levels = [lax.all_gather(top.T, AXES, axis=0, tiled=False)]
    for height in range(log_dev - 4):
        coeffs = levels[-1]
        pairs = coeffs.reshape(coeffs.shape[0] // 2, 2, coeffs.shape[1], coeffs.shape[2])
        levels.append(
            jnp.einsum("cprj,pjk->crk", pairs, transfer[LOG_LD + height], precision=highest)
        )
    reach = max(OFFSETS)
    picks = [reach + offset for offset in OFFSETS]
    windows = []
    for height in range(log_dev - 3):
        coeffs = levels[height]
        clusters = coeffs.shape[0]
        cluster = device_index // 2**height
        padded = jnp.pad(coeffs, ((reach, reach), (0, 0), (0, 0)))
        window = lax.dynamic_slice_in_dim(padded, cluster, 2 * reach + 1, axis=0)
        window = jnp.concatenate([window[: picks[3] + 1], window[picks[4] :]], axis=0)
        mask_row = 2 * device_count - 2 * clusters + cluster
        live_slots = lax.dynamic_index_in_dim(upper_mask, mask_row, 1, keepdims=False).astype(
            jnp.float32
        )
        weights = jnp.stack(slot_weights(live_slots, (cluster % 2 == 0).astype(jnp.float32)))
        windows.append(window * weights[:, None, None])
    stacked = jnp.stack(windows)
    coupled = jnp.einsum(
        "hpij,hprj->hri", coupling[LOG_LD : LOG_LD + log_dev - 3], stacked, precision=highest
    )
    far_field = coupled[-1]
    for height in range(log_dev - 5, -1, -1):
        side_bit = device_index // 2**height % 2
        far_field = coupled[height] + jnp.einsum(
            "rj,kj->rk", far_field, transfer[LOG_LD + height][side_bit], precision=highest
        )
    return far_field.T


def local(
    charge_input,
    points,
    tree_order,
    cluster_basis,
    near_mask,
    lower_mask,
    upper_mask,
    transfer,
    coupling,
):
    device_count = lax.axis_size(AXES)
    device_index = lax.axis_index(AXES)
    tree_positions = tree_order[0]
    right_sides = charge_input.shape[0]
    stacked = jnp.concatenate([charge_input, points], axis=0)[:, tree_positions]
    charges = stacked[:right_sides]
    rows, width = stacked.shape[0], 3 * LS
    leaf_basis = cluster_basis.reshape(K, LEAF_DEV, LS)
    upward = [
        jnp.einsum(
            "kla,rla->klr",
            leaf_basis,
            charges.reshape(right_sides, LEAF_DEV, LS),
            precision=highest,
        )
    ]
    for tree_level in range(LOG_LD):
        coeffs = upward[-1]
        upward.append(raise_pairs(transfer[tree_level], coeffs))
    left_parts = [[], [], [], []]
    right_parts = [[], [], [], []]
    for tree_level in range(LOG_LD):
        coeffs = upward[tree_level]
        clusters = coeffs.shape[1]
        for distance in range(1, -(-6 // clusters) + 1):
            left_parts[distance].append(coeffs[:, max(0, distance * clusters - 6) :])
            right_parts[distance].append(coeffs[:, : min(clusters, 6 - (distance - 1) * clusters)])
    from_left = [None, None, None, None]
    from_right = [None, None, None, None]
    halo_size = rows * width
    for distance in range(1, 4):
        packed_left = jnp.concatenate(left_parts[distance], axis=1)
        packed_right = jnp.concatenate(right_parts[distance], axis=1)
        if distance == 1:
            flat_left = jnp.concatenate(
                [stacked[:, -width:].reshape(-1), packed_left.reshape(-1)]
            )
            flat_right = jnp.concatenate(
                [stacked[:, :width].reshape(-1), packed_right.reshape(-1)]
            )
            got_left = exchange(flat_left, 1)
            got_right = exchange(flat_right, -1)
            halo_before = got_left[:halo_size].reshape(rows, width)
            halo_after = got_right[:halo_size].reshape(rows, width)
            from_left[1] = got_left[halo_size:].reshape(packed_left.shape)
            from_right[1] = got_right[halo_size:].reshape(packed_right.shape)
        else:
            from_left[distance] = exchange(packed_left, distance)
            from_right[distance] = exchange(packed_right, -distance)
    widened = jnp.concatenate([halo_before, stacked, halo_after], axis=1)
    near_part = near_field(widened[:right_sides], widened[right_sides:], near_mask)
    cursors_left = [0, 0, 0, 0]
    cursors_right = [0, 0, 0, 0]
    coupled_local = []
    for tree_level in range(LOG_LD):
        coeffs = upward[tree_level]
        clusters = coeffs.shape[1]
        reach_devices = -(-6 // clusters)
        before = []
        beyond = []
        for distance in range(reach_devices, 0, -1):
            piece_width = clusters - max(0, distance * clusters - 6)
            before.append(
                from_left[distance][
                    :, cursors_left[distance] : cursors_left[distance] + piece_width
                ]
            )
            cursors_left[distance] += piece_width
        for distance in range(1, reach_devices + 1):
            piece_width = min(clusters, 6 - (distance - 1) * clusters)
            beyond.append(
                from_right[distance][
                    :, cursors_right[distance] : cursors_right[distance] + piece_width
                ]
            )
            cursors_right[distance] += piece_width
        padded = jnp.concatenate(before + [coeffs] + beyond, axis=1)
        first_row = 2 * LEAF_DEV - 2 * clusters
        live_slots = lower_mask[0][:, first_row : first_row + clusters].astype(jnp.float32)
        is_even = (jnp.arange(clusters) % 2 == 0).astype(jnp.float32)
        coupled_local.append(
            couple_window(padded, coupling[tree_level], slot_weights(live_slots, is_even), 6)
        )
    far_field = upper_far_field(
        upward[LOG_LD][:, 0], device_index, device_count, upper_mask, transfer, coupling
    )
    far_field = far_field[:, None, :]
    for tree_level in range(LOG_LD - 1, -1, -1):
        far_field = coupled_local[tree_level] + lower_pairs(transfer[tree_level], far_field)
    far_part = jnp.einsum("klr,kla->rla", far_field, leaf_basis, precision=highest).reshape(
        right_sides, LEAF_DEV * LS
    )
    potential_tree = near_part + far_part
    return jnp.zeros_like(potential_tree).at[:, tree_positions].set(potential_tree)


def solution(mesh):
    placed = (
        P(None, ("group", "leaf")),
        P(None, ("group", "leaf")),
        P(("group", "leaf"), None),
        P(None, ("group", "leaf")),
        P(None, ("group", "leaf")),
        P(("group", "leaf"), None, None),
        P(),
        P(),
        P(),
    )
    return jax.shard_map(
        local, mesh=mesh, in_specs=placed, out_specs=P(None, ("group", "leaf")), check_vma=False
    )
```

```python
import jax
import jax.numpy as jnp
from jax import lax
from jax.sharding import PartitionSpec as P

K = 64
LS = 64
LEAF_DEV = 32
LOG_LD = 5


KERNEL_SCALE = 0.0625
SOFTENING = 0.01
OFFSETS = (-7, -6, -5, -4, 4, 5, 6, 7)
highest = lax.Precision.HIGHEST


def from_behind(shard, axis, by):
    peers = lax.axis_size(axis)
    pairs = [(i, i + by) for i in range(peers) if 0 <= i + by < peers]
    return lax.ppermute(shard, axis, pairs)


def extended_2(shard, sides, width):
    for axis, dim in sides:
        peers, length = (lax.axis_size(axis), shard.shape[dim])
        up = [(i, (i + 1) % peers) for i in range(peers - 1)]
        down = [(j, i) for i, j in up]
        last = lax.slice_in_dim(shard, length - width, length, axis=dim)
        first = lax.slice_in_dim(shard, 0, width, axis=dim)
        before = lax.ppermute(last, axis, up)
        after = lax.ppermute(first, axis, down)
        shard = jnp.concatenate([before, shard, after], axis=dim)
    return shard


def from_partner(block, axis, stride):
    count = lax.axis_size(axis)
    route = []
    for low in range(count):
        high = low | 1 << stride
        if high != low and high < count:
            route += [(low, high), (high, low)]
    return lax.ppermute(block, axis, route)


def near_field(charge_window, point_window, near_mask):
    leaves = near_mask.shape[1]
    right_sides = charge_window.shape[0]
    offsets = (-3, -2, -1, 0, 1, 2, 3)
    point_grid = point_window.reshape(3, leaves + 6, LS)
    target = point_grid[:, 3 : 3 + leaves]
    sources = jnp.stack([point_grid[:, 3 + o : 3 + o + leaves] for o in offsets], axis=2)
    separation = target[:, :, None, :, None] - sources[:, :, :, None, :]
    ones = jnp.ones((1, leaves), jnp.float32)
    masks = near_mask.astype(jnp.float32)
    weight = jnp.concatenate([masks[:3], ones, masks[3:]], axis=0).T
    kernel = KERNEL_SCALE * lax.rsqrt(jnp.sum(separation * separation, axis=0) + SOFTENING)
    kernel = kernel * weight[:, :, None, None]
    kernel = kernel.transpose(0, 2, 1, 3).reshape(leaves, LS, len(offsets) * LS)
    charge_grid = charge_window.reshape(right_sides, leaves + 6, LS).transpose(1, 2, 0)
    charges = jnp.stack([charge_grid[3 + o : 3 + o + leaves] for o in offsets], axis=1)
    charges = charges.reshape(leaves, len(offsets) * LS, right_sides)
    summed = jnp.einsum("lab,lbr->lar", kernel, charges, precision=highest)
    return summed.transpose(2, 0, 1).reshape(right_sides, leaves * LS)


def slot_weights(live_slots, is_even):
    is_odd = 1.0 - is_even
    return (
        live_slots[6] * is_odd,
        live_slots[0],
        live_slots[1],
        live_slots[2],
        live_slots[3],
        live_slots[4],
        live_slots[5],
        live_slots[6] * is_even,
    )


def couple_window(padded, coupling_table, weights, reach_cells):
    clusters = padded.shape[1] - 2 * reach_cells
    extended = jnp.pad(padded, ((0, 0), (1, 1), (0, 0)))
    products = jnp.einsum("pij,jmr->pimr", coupling_table, extended, precision=highest)
    summed = None
    for position, offset in enumerate(OFFSETS):
        first_col = reach_cells + 1 + offset
        term = products[position, :, first_col : first_col + clusters] * weights[position][None, :, None]
        summed = term if summed is None else summed + term
    return summed


def raise_pairs(table, coeffs):
    pairs = coeffs.reshape(coeffs.shape[0], coeffs.shape[1] // 2, 2, coeffs.shape[2])
    return jnp.einsum("pjk,jcpr->kcr", table, pairs, precision=highest)


def lower_pairs(table, coeffs):
    children = jnp.einsum("pkj,jnr->knpr", table, coeffs, precision=highest)
    return children.reshape(coeffs.shape[0], 2 * coeffs.shape[1], coeffs.shape[2])


def raise_level(matrix, coeffs):
    return jnp.einsum("jk,jnr->knr", matrix, coeffs, precision=highest)


def lower_level(matrix, coeffs):
    return jnp.einsum("kj,jnr->knr", matrix, coeffs, precision=highest)


def alternate_children(first_child, second_child):
    stacked = jnp.stack([first_child, second_child], axis=2)
    return stacked.reshape(first_child.shape[0], 2 * first_child.shape[1], first_child.shape[2])


AXES = ("group", "leaf")


def exchange(shard, by):
    return from_behind(shard, AXES, by)


def upper_far_field(top, device_index, device_count, upper_mask, transfer, coupling):
    log_dev = device_count.bit_length() - 1
    levels = [lax.all_gather(top.T, AXES, axis=0, tiled=False)]
    for height in range(log_dev - 4):
        coeffs = levels[-1]
        clusters, right_sides = coeffs.shape[0], coeffs.shape[1]
        pairs = coeffs.reshape(clusters // 2, 2, right_sides, K).transpose(0, 2, 1, 3)
        pairs = pairs.reshape(clusters // 2 * right_sides, 2 * K)
        raised = jnp.dot(pairs, transfer[LOG_LD + height].reshape(2 * K, K), precision=highest)
        levels.append(raised.reshape(clusters // 2, right_sides, K))
    reach = max(OFFSETS)
    picks = [reach + offset for offset in OFFSETS]
    windows = []
    for height in range(log_dev - 3):
        coeffs = levels[height]
        clusters = coeffs.shape[0]
        cluster = device_index // 2**height
        padded = jnp.pad(coeffs, ((reach, reach), (0, 0), (0, 0)))
        window = lax.dynamic_slice_in_dim(padded, cluster, 2 * reach + 1, axis=0)
        window = jnp.concatenate([window[: picks[3] + 1], window[picks[4] :]], axis=0)
        mask_row = 2 * device_count - 2 * clusters + cluster
        live_slots = lax.dynamic_index_in_dim(upper_mask, mask_row, 1, keepdims=False).astype(
            jnp.float32
        )
        weights = jnp.stack(slot_weights(live_slots, (cluster % 2 == 0).astype(jnp.float32)))
        windows.append(window * weights[:, None, None])
    stacked = jnp.stack(windows)
    coupled = jnp.einsum(
        "hpij,hprj->hri", coupling[LOG_LD : LOG_LD + log_dev - 3], stacked, precision=highest
    )
    far_field = coupled[-1]
    for height in range(log_dev - 5, -1, -1):
        side_bit = device_index // 2**height % 2
        far_field = coupled[height] + jnp.einsum(
            "rj,kj->rk", far_field, transfer[LOG_LD + height][side_bit], precision=highest
        )
    return far_field.T


def local(
    charge_input,
    points,
    tree_order,
    cluster_basis,
    near_mask,
    lower_mask,
    upper_mask,
    transfer,
    coupling,
):
    device_count = lax.axis_size(AXES)
    device_index = lax.axis_index(AXES)
    tree_positions = tree_order[0]
    right_sides = charge_input.shape[0]
    stacked = jnp.concatenate([charge_input, points], axis=0)[:, tree_positions]
    charges = stacked[:right_sides]
    rows, width = stacked.shape[0], 3 * LS
    leaf_basis = cluster_basis.reshape(K, LEAF_DEV, LS)
    upward = [
        jnp.einsum(
            "kla,rla->klr",
            leaf_basis,
            charges.reshape(right_sides, LEAF_DEV, LS),
            precision=highest,
        )
    ]
    for tree_level in range(LOG_LD):
        coeffs = upward[-1]
        upward.append(raise_pairs(transfer[tree_level], coeffs))
    left_parts = [[], [], [], []]
    right_parts = [[], [], [], []]
    for tree_level in range(LOG_LD):
        coeffs = upward[tree_level]
        clusters = coeffs.shape[1]
        for distance in range(1, -(-6 // clusters) + 1):
            left_parts[distance].append(coeffs[:, max(0, distance * clusters - 6) :])
            right_parts[distance].append(coeffs[:, : min(clusters, 6 - (distance - 1) * clusters)])
    from_left = [None, None, None, None]
    from_right = [None, None, None, None]
    halo_size = rows * width
    for distance in range(1, 4):
        packed_left = jnp.concatenate(left_parts[distance], axis=1)
        packed_right = jnp.concatenate(right_parts[distance], axis=1)
        if distance == 1:
            flat_left = jnp.concatenate(
                [stacked[:, -width:].reshape(-1), packed_left.reshape(-1)]
            )
            flat_right = jnp.concatenate(
                [stacked[:, :width].reshape(-1), packed_right.reshape(-1)]
            )
            got_left = exchange(flat_left, 1)
            got_right = exchange(flat_right, -1)
            halo_before = got_left[:halo_size].reshape(rows, width)
            halo_after = got_right[:halo_size].reshape(rows, width)
            from_left[1] = got_left[halo_size:].reshape(packed_left.shape)
            from_right[1] = got_right[halo_size:].reshape(packed_right.shape)
        else:
            from_left[distance] = exchange(packed_left, distance)
            from_right[distance] = exchange(packed_right, -distance)
    widened = jnp.concatenate([halo_before, stacked, halo_after], axis=1)
    near_part = near_field(widened[:right_sides], widened[right_sides:], near_mask)
    cursors_left = [0, 0, 0, 0]
    cursors_right = [0, 0, 0, 0]
    coupled_local = []
    for tree_level in range(LOG_LD):
        coeffs = upward[tree_level]
        clusters = coeffs.shape[1]
        reach_devices = -(-6 // clusters)
        before = []
        beyond = []
        for distance in range(reach_devices, 0, -1):
            piece_width = clusters - max(0, distance * clusters - 6)
            before.append(
                from_left[distance][
                    :, cursors_left[distance] : cursors_left[distance] + piece_width
                ]
            )
            cursors_left[distance] += piece_width
        for distance in range(1, reach_devices + 1):
            piece_width = min(clusters, 6 - (distance - 1) * clusters)
            beyond.append(
                from_right[distance][
                    :, cursors_right[distance] : cursors_right[distance] + piece_width
                ]
            )
            cursors_right[distance] += piece_width
        padded = jnp.concatenate(before + [coeffs] + beyond, axis=1)
        first_row = 2 * LEAF_DEV - 2 * clusters
        live_slots = lower_mask[0][:, first_row : first_row + clusters].astype(jnp.float32)
        is_even = (jnp.arange(clusters) % 2 == 0).astype(jnp.float32)
        coupled_local.append(
            couple_window(padded, coupling[tree_level], slot_weights(live_slots, is_even), 6)
        )
    far_field = upper_far_field(
        upward[LOG_LD][:, 0], device_index, device_count, upper_mask, transfer, coupling
    )
    far_field = far_field[:, None, :]
    for tree_level in range(LOG_LD - 1, -1, -1):
        far_field = coupled_local[tree_level] + lower_pairs(transfer[tree_level], far_field)
    far_part = jnp.einsum("klr,kla->rla", far_field, leaf_basis, precision=highest).reshape(
        right_sides, LEAF_DEV * LS
    )
    potential_tree = near_part + far_part
    return jnp.zeros_like(potential_tree).at[:, tree_positions].set(potential_tree)


def solution(mesh):
    placed = (
        P(None, ("group", "leaf")),
        P(None, ("group", "leaf")),
        P(("group", "leaf"), None),
        P(None, ("group", "leaf")),
        P(None, ("group", "leaf")),
        P(("group", "leaf"), None, None),
        P(),
        P(),
        P(),
    )
    return jax.shard_map(
        local, mesh=mesh, in_specs=placed, out_specs=P(None, ("group", "leaf")), check_vma=False
    )
```

```python
import jax
import jax.numpy as jnp
from jax import lax
from jax.sharding import PartitionSpec as P
from jax.experimental import pallas as pl
from jax.experimental.pallas import tpu as pltpu

K = 64
LS = 64
LEAF_DEV = 32
LOG_LD = 5


KERNEL_SCALE = 0.0625
SOFTENING = 0.01
OFFSETS = (-7, -6, -5, -4, 4, 5, 6, 7)
highest = lax.Precision.HIGHEST


def from_behind(shard, axis, by):
    peers = lax.axis_size(axis)
    pairs = [(i, i + by) for i in range(peers) if 0 <= i + by < peers]
    return lax.ppermute(shard, axis, pairs)


def extended_2(shard, sides, width):
    for axis, dim in sides:
        peers, length = (lax.axis_size(axis), shard.shape[dim])
        up = [(i, (i + 1) % peers) for i in range(peers - 1)]
        down = [(j, i) for i, j in up]
        last = lax.slice_in_dim(shard, length - width, length, axis=dim)
        first = lax.slice_in_dim(shard, 0, width, axis=dim)
        before = lax.ppermute(last, axis, up)
        after = lax.ppermute(first, axis, down)
        shard = jnp.concatenate([before, shard, after], axis=dim)
    return shard


def from_partner(block, axis, stride):
    count = lax.axis_size(axis)
    route = []
    for low in range(count):
        high = low | 1 << stride
        if high != low and high < count:
            route += [(low, high), (high, low)]
    return lax.ppermute(block, axis, route)


NEAR_REACH = 3


def near_kernel(charge_ref, point_ref, column_ref, weight_ref, out_ref):
    leaves = weight_ref.shape[0]
    span = (2 * NEAR_REACH + 1) * LS
    blocks = []
    for leaf in range(leaves):
        first = leaf * LS
        source = column_ref[first : first + span, :]
        squared = None
        for axis in range(3):
            target = point_ref[axis : axis + 1, first + NEAR_REACH * LS : first + (NEAR_REACH + 1) * LS]
            gap = source[:, axis : axis + 1] - target
            squared = gap * gap if squared is None else squared + gap * gap
        kernel = KERNEL_SCALE * lax.rsqrt(squared + SOFTENING)
        charges = charge_ref[:, first : first + span] * weight_ref[leaf : leaf + 1, :]
        blocks.append(
            jnp.dot(charges, kernel, precision=highest, preferred_element_type=jnp.float32)
        )
    out_ref[...] = jnp.concatenate(blocks, axis=1)


def near_field(charge_window, point_window, near_mask):
    leaves = near_mask.shape[1]
    right_sides = charge_window.shape[0]
    masks = near_mask.astype(jnp.float32)
    ones = jnp.ones((1, leaves), jnp.float32)
    weight = jnp.concatenate([masks[:NEAR_REACH], ones, masks[NEAR_REACH:]], axis=0).T
    weight = jnp.repeat(weight, LS, axis=1)
    whole = pl.BlockSpec(memory_space=pltpu.VMEM)
    return pl.pallas_call(
        near_kernel,
        out_shape=jax.ShapeDtypeStruct((right_sides, leaves * LS), jnp.float32),
        in_specs=[whole] * 4,
        out_specs=whole,
        cost_estimate=pl.CostEstimate(
            flops=2 * right_sides * leaves * LS * (2 * NEAR_REACH + 1) * LS * 6,
            transcendentals=leaves * LS * (2 * NEAR_REACH + 1) * LS,
            bytes_accessed=4 * (right_sides + 6) * (leaves + 6) * LS + 4 * right_sides * leaves * LS,
        ),
    )(charge_window, point_window, point_window.T, weight)


def slot_weights(live_slots, is_even):
    is_odd = 1.0 - is_even
    return (
        live_slots[6] * is_odd,
        live_slots[0],
        live_slots[1],
        live_slots[2],
        live_slots[3],
        live_slots[4],
        live_slots[5],
        live_slots[6] * is_even,
    )


def couple_window(padded, coupling_table, weights, reach_cells):
    clusters = padded.shape[1] - 2 * reach_cells
    extended = jnp.pad(padded, ((0, 0), (1, 1), (0, 0)))
    products = jnp.einsum("pij,jmr->pimr", coupling_table, extended, precision=highest)
    summed = None
    for position, offset in enumerate(OFFSETS):
        first_col = reach_cells + 1 + offset
        term = products[position, :, first_col : first_col + clusters] * weights[position][None, :, None]
        summed = term if summed is None else summed + term
    return summed


def raise_pairs(table, coeffs):
    pairs = coeffs.reshape(coeffs.shape[0], coeffs.shape[1] // 2, 2, coeffs.shape[2])
    return jnp.einsum("pjk,jcpr->kcr", table, pairs, precision=highest)


def lower_pairs(table, coeffs):
    children = jnp.einsum("pkj,jnr->knpr", table, coeffs, precision=highest)
    return children.reshape(coeffs.shape[0], 2 * coeffs.shape[1], coeffs.shape[2])


def raise_level(matrix, coeffs):
    return jnp.einsum("jk,jnr->knr", matrix, coeffs, precision=highest)


def lower_level(matrix, coeffs):
    return jnp.einsum("kj,jnr->knr", matrix, coeffs, precision=highest)


def alternate_children(first_child, second_child):
    stacked = jnp.stack([first_child, second_child], axis=2)
    return stacked.reshape(first_child.shape[0], 2 * first_child.shape[1], first_child.shape[2])


AXES = ("group", "leaf")


def exchange(shard, by):
    return from_behind(shard, AXES, by)


def upper_far_field(top, device_index, device_count, upper_mask, transfer, coupling):
    log_dev = device_count.bit_length() - 1
    levels = [lax.all_gather(top.T, AXES, axis=0, tiled=False)]
    for height in range(log_dev - 4):
        coeffs = levels[-1]
        pairs = coeffs.reshape(coeffs.shape[0] // 2, 2, coeffs.shape[1], coeffs.shape[2])
        levels.append(
            jnp.einsum("cprj,pjk->crk", pairs, transfer[LOG_LD + height], precision=highest)
        )
    reach = max(OFFSETS)
    picks = [reach + offset for offset in OFFSETS]
    windows = []
    for height in range(log_dev - 3):
        coeffs = levels[height]
        clusters = coeffs.shape[0]
        cluster = device_index // 2**height
        padded = jnp.pad(coeffs, ((reach, reach), (0, 0), (0, 0)))
        window = lax.dynamic_slice_in_dim(padded, cluster, 2 * reach + 1, axis=0)
        window = jnp.concatenate([window[: picks[3] + 1], window[picks[4] :]], axis=0)
        mask_row = 2 * device_count - 2 * clusters + cluster
        live_slots = lax.dynamic_index_in_dim(upper_mask, mask_row, 1, keepdims=False).astype(
            jnp.float32
        )
        weights = jnp.stack(slot_weights(live_slots, (cluster % 2 == 0).astype(jnp.float32)))
        windows.append(window * weights[:, None, None])
    stacked = jnp.stack(windows)
    coupled = jnp.einsum(
        "hpij,hprj->hri", coupling[LOG_LD : LOG_LD + log_dev - 3], stacked, precision=highest
    )
    far_field = coupled[-1]
    for height in range(log_dev - 5, -1, -1):
        side_bit = device_index // 2**height % 2
        far_field = coupled[height] + jnp.einsum(
            "rj,kj->rk", far_field, transfer[LOG_LD + height][side_bit], precision=highest
        )
    return far_field.T


def local(
    charge_input,
    points,
    tree_order,
    cluster_basis,
    near_mask,
    lower_mask,
    upper_mask,
    transfer,
    coupling,
):
    device_count = lax.axis_size(AXES)
    device_index = lax.axis_index(AXES)
    tree_positions = tree_order[0]
    right_sides = charge_input.shape[0]
    stacked = jnp.concatenate([charge_input, points], axis=0)[:, tree_positions]
    charges = stacked[:right_sides]
    rows, width = stacked.shape[0], 3 * LS
    leaf_basis = cluster_basis.reshape(K, LEAF_DEV, LS)
    upward = [
        jnp.einsum(
            "kla,rla->klr",
            leaf_basis,
            charges.reshape(right_sides, LEAF_DEV, LS),
            precision=highest,
        )
    ]
    for tree_level in range(LOG_LD):
        coeffs = upward[-1]
        upward.append(raise_pairs(transfer[tree_level], coeffs))
    left_parts = [[], [], [], []]
    right_parts = [[], [], [], []]
    for tree_level in range(LOG_LD):
        coeffs = upward[tree_level]
        clusters = coeffs.shape[1]
        for distance in range(1, -(-6 // clusters) + 1):
            left_parts[distance].append(coeffs[:, max(0, distance * clusters - 6) :])
            right_parts[distance].append(coeffs[:, : min(clusters, 6 - (distance - 1) * clusters)])
    from_left = [None, None, None, None]
    from_right = [None, None, None, None]
    halo_size = rows * width
    for distance in range(1, 4):
        packed_left = jnp.concatenate(left_parts[distance], axis=1)
        packed_right = jnp.concatenate(right_parts[distance], axis=1)
        if distance == 1:
            flat_left = jnp.concatenate(
                [stacked[:, -width:].reshape(-1), packed_left.reshape(-1)]
            )
            flat_right = jnp.concatenate(
                [stacked[:, :width].reshape(-1), packed_right.reshape(-1)]
            )
            got_left = exchange(flat_left, 1)
            got_right = exchange(flat_right, -1)
            halo_before = got_left[:halo_size].reshape(rows, width)
            halo_after = got_right[:halo_size].reshape(rows, width)
            from_left[1] = got_left[halo_size:].reshape(packed_left.shape)
            from_right[1] = got_right[halo_size:].reshape(packed_right.shape)
        else:
            from_left[distance] = exchange(packed_left, distance)
            from_right[distance] = exchange(packed_right, -distance)
    widened = jnp.concatenate([halo_before, stacked, halo_after], axis=1)
    near_part = near_field(widened[:right_sides], widened[right_sides:], near_mask)
    cursors_left = [0, 0, 0, 0]
    cursors_right = [0, 0, 0, 0]
    coupled_local = []
    for tree_level in range(LOG_LD):
        coeffs = upward[tree_level]
        clusters = coeffs.shape[1]
        reach_devices = -(-6 // clusters)
        before = []
        beyond = []
        for distance in range(reach_devices, 0, -1):
            piece_width = clusters - max(0, distance * clusters - 6)
            before.append(
                from_left[distance][
                    :, cursors_left[distance] : cursors_left[distance] + piece_width
                ]
            )
            cursors_left[distance] += piece_width
        for distance in range(1, reach_devices + 1):
            piece_width = min(clusters, 6 - (distance - 1) * clusters)
            beyond.append(
                from_right[distance][
                    :, cursors_right[distance] : cursors_right[distance] + piece_width
                ]
            )
            cursors_right[distance] += piece_width
        padded = jnp.concatenate(before + [coeffs] + beyond, axis=1)
        first_row = 2 * LEAF_DEV - 2 * clusters
        live_slots = lower_mask[0][:, first_row : first_row + clusters].astype(jnp.float32)
        is_even = (jnp.arange(clusters) % 2 == 0).astype(jnp.float32)
        coupled_local.append(
            couple_window(padded, coupling[tree_level], slot_weights(live_slots, is_even), 6)
        )
    far_field = upper_far_field(
        upward[LOG_LD][:, 0], device_index, device_count, upper_mask, transfer, coupling
    )
    far_field = far_field[:, None, :]
    for tree_level in range(LOG_LD - 1, -1, -1):
        far_field = coupled_local[tree_level] + lower_pairs(transfer[tree_level], far_field)
    far_part = jnp.einsum("klr,kla->rla", far_field, leaf_basis, precision=highest).reshape(
        right_sides, LEAF_DEV * LS
    )
    potential_tree = near_part + far_part
    return jnp.zeros_like(potential_tree).at[:, tree_positions].set(potential_tree)


def solution(mesh):
    placed = (
        P(None, ("group", "leaf")),
        P(None, ("group", "leaf")),
        P(("group", "leaf"), None),
        P(None, ("group", "leaf")),
        P(None, ("group", "leaf")),
        P(("group", "leaf"), None, None),
        P(),
        P(),
        P(),
    )
    return jax.shard_map(
        local, mesh=mesh, in_specs=placed, out_specs=P(None, ("group", "leaf")), check_vma=False
    )
```

```python
import jax
import jax.numpy as jnp
from jax import lax
from jax.sharding import PartitionSpec as P
from jax.experimental import pallas as pl
from jax.experimental.pallas import tpu as pltpu

K = 64
LS = 64
LEAF_DEV = 32
LOG_LD = 5


KERNEL_SCALE = 0.0625
SOFTENING = 0.01
OFFSETS = (-7, -6, -5, -4, 4, 5, 6, 7)
highest = lax.Precision.HIGHEST


def from_behind(shard, axis, by):
    peers = lax.axis_size(axis)
    pairs = [(i, i + by) for i in range(peers) if 0 <= i + by < peers]
    return lax.ppermute(shard, axis, pairs)


def extended_2(shard, sides, width):
    for axis, dim in sides:
        peers, length = (lax.axis_size(axis), shard.shape[dim])
        up = [(i, (i + 1) % peers) for i in range(peers - 1)]
        down = [(j, i) for i, j in up]
        last = lax.slice_in_dim(shard, length - width, length, axis=dim)
        first = lax.slice_in_dim(shard, 0, width, axis=dim)
        before = lax.ppermute(last, axis, up)
        after = lax.ppermute(first, axis, down)
        shard = jnp.concatenate([before, shard, after], axis=dim)
    return shard


def from_partner(block, axis, stride):
    count = lax.axis_size(axis)
    route = []
    for low in range(count):
        high = low | 1 << stride
        if high != low and high < count:
            route += [(low, high), (high, low)]
    return lax.ppermute(block, axis, route)


NEAR_REACH = 3


def near_kernel(charge_ref, point_ref, column_ref, weight_ref, out_ref):
    leaves = weight_ref.shape[0]
    span = (2 * NEAR_REACH + 1) * LS
    blocks = []
    for leaf in range(leaves):
        first = leaf * LS
        source = column_ref[first : first + span, :]
        squared = None
        for axis in range(3):
            target = point_ref[axis : axis + 1, first + NEAR_REACH * LS : first + (NEAR_REACH + 1) * LS]
            gap = source[:, axis : axis + 1] - target
            squared = gap * gap if squared is None else squared + gap * gap
        kernel = KERNEL_SCALE * lax.rsqrt(squared + SOFTENING)
        charges = charge_ref[:, first : first + span] * weight_ref[leaf : leaf + 1, :]
        blocks.append(
            jnp.dot(charges, kernel, precision=highest, preferred_element_type=jnp.float32)
        )
    out_ref[...] = jnp.concatenate(blocks, axis=1)


def near_field(charge_window, point_window, near_mask):
    leaves = near_mask.shape[1]
    right_sides = charge_window.shape[0]
    masks = near_mask.astype(jnp.float32)
    ones = jnp.ones((1, leaves), jnp.float32)
    weight = jnp.concatenate([masks[:NEAR_REACH], ones, masks[NEAR_REACH:]], axis=0).T
    weight = jnp.repeat(weight, LS, axis=1)
    whole = pl.BlockSpec(memory_space=pltpu.VMEM)
    return pl.pallas_call(
        near_kernel,
        out_shape=jax.ShapeDtypeStruct((right_sides, leaves * LS), jnp.float32),
        in_specs=[whole] * 4,
        out_specs=whole,
        cost_estimate=pl.CostEstimate(
            flops=2 * right_sides * leaves * LS * (2 * NEAR_REACH + 1) * LS * 6,
            transcendentals=leaves * LS * (2 * NEAR_REACH + 1) * LS,
            bytes_accessed=4 * (right_sides + 6) * (leaves + 6) * LS + 4 * right_sides * leaves * LS,
        ),
    )(charge_window, point_window, point_window.T, weight)


def slot_weights(live_slots, is_even):
    is_odd = 1.0 - is_even
    return (
        live_slots[6] * is_odd,
        live_slots[0],
        live_slots[1],
        live_slots[2],
        live_slots[3],
        live_slots[4],
        live_slots[5],
        live_slots[6] * is_even,
    )


def couple_window(padded, coupling_table, weights, reach_cells):
    clusters = padded.shape[1] - 2 * reach_cells
    extended = jnp.pad(padded, ((0, 0), (1, 1), (0, 0)))
    products = jnp.einsum("pij,jmr->pimr", coupling_table, extended, precision=highest)
    summed = None
    for position, offset in enumerate(OFFSETS):
        first_col = reach_cells + 1 + offset
        term = products[position, :, first_col : first_col + clusters] * weights[position][None, :, None]
        summed = term if summed is None else summed + term
    return summed


def raise_pairs(table, coeffs):
    pairs = coeffs.reshape(coeffs.shape[0], coeffs.shape[1] // 2, 2, coeffs.shape[2])
    return jnp.einsum("pjk,jcpr->kcr", table, pairs, precision=highest)


def lower_pairs(table, coeffs):
    children = jnp.einsum("pkj,jnr->knpr", table, coeffs, precision=highest)
    return children.reshape(coeffs.shape[0], 2 * coeffs.shape[1], coeffs.shape[2])


def raise_level(matrix, coeffs):
    return jnp.einsum("jk,jnr->knr", matrix, coeffs, precision=highest)


def lower_level(matrix, coeffs):
    return jnp.einsum("kj,jnr->knr", matrix, coeffs, precision=highest)


def alternate_children(first_child, second_child):
    stacked = jnp.stack([first_child, second_child], axis=2)
    return stacked.reshape(first_child.shape[0], 2 * first_child.shape[1], first_child.shape[2])


AXES = ("group", "leaf")


def exchange(shard, by):
    return from_behind(shard, AXES, by)


def upper_far_field(top, device_index, device_count, upper_mask, transfer, coupling):
    log_dev = device_count.bit_length() - 1
    within = lax.all_gather(top.T, AXES[1], axis=0, tiled=False)
    gathered = lax.all_gather(within, AXES[0], axis=0, tiled=False)
    levels = [gathered.reshape(device_count, top.shape[1], top.shape[0])]
    for height in range(log_dev - 4):
        coeffs = levels[-1]
        clusters, right_sides = coeffs.shape[0], coeffs.shape[1]
        pairs = coeffs.reshape(clusters // 2, 2, right_sides, K)
        even = pairs[:, 0].reshape(clusters // 2 * right_sides, K)
        odd = pairs[:, 1].reshape(clusters // 2 * right_sides, K)
        table = transfer[LOG_LD + height]
        raised = jnp.dot(even, table[0], precision=highest) + jnp.dot(odd, table[1], precision=highest)
        levels.append(raised.reshape(clusters // 2, right_sides, K))
    reach = max(OFFSETS)
    picks = [reach + offset for offset in OFFSETS]
    windows = []
    for height in range(log_dev - 3):
        coeffs = levels[height]
        clusters = coeffs.shape[0]
        cluster = device_index // 2**height
        padded = jnp.pad(coeffs, ((reach, reach), (0, 0), (0, 0)))
        window = lax.dynamic_slice_in_dim(padded, cluster, 2 * reach + 1, axis=0)
        window = jnp.concatenate([window[: picks[3] + 1], window[picks[4] :]], axis=0)
        mask_row = 2 * device_count - 2 * clusters + cluster
        live_slots = lax.dynamic_index_in_dim(upper_mask, mask_row, 1, keepdims=False).astype(
            jnp.float32
        )
        weights = jnp.stack(slot_weights(live_slots, (cluster % 2 == 0).astype(jnp.float32)))
        windows.append(window * weights[:, None, None])
    stacked = jnp.stack(windows)
    coupled = jnp.einsum(
        "hpij,hprj->hri", coupling[LOG_LD : LOG_LD + log_dev - 3], stacked, precision=highest
    )
    far_field = coupled[-1]
    for height in range(log_dev - 5, -1, -1):
        side_bit = device_index // 2**height % 2
        far_field = coupled[height] + jnp.einsum(
            "rj,kj->rk", far_field, transfer[LOG_LD + height][side_bit], precision=highest
        )
    return far_field.T


def local(
    charge_input,
    points,
    tree_order,
    cluster_basis,
    near_mask,
    lower_mask,
    upper_mask,
    transfer,
    coupling,
):
    device_count = lax.axis_size(AXES)
    device_index = lax.axis_index(AXES)
    tree_positions = tree_order[0]
    right_sides = charge_input.shape[0]
    stacked = jnp.concatenate([charge_input, points], axis=0)[:, tree_positions]
    charges = stacked[:right_sides]
    rows, width = stacked.shape[0], 3 * LS
    leaf_basis = cluster_basis.reshape(K, LEAF_DEV, LS)
    upward = [
        jnp.einsum(
            "kla,rla->klr",
            leaf_basis,
            charges.reshape(right_sides, LEAF_DEV, LS),
            precision=highest,
        )
    ]
    for tree_level in range(LOG_LD):
        coeffs = upward[-1]
        upward.append(raise_pairs(transfer[tree_level], coeffs))
    left_parts = [[], [], [], []]
    right_parts = [[], [], [], []]
    for tree_level in range(LOG_LD):
        coeffs = upward[tree_level]
        clusters = coeffs.shape[1]
        for distance in range(1, -(-6 // clusters) + 1):
            left_parts[distance].append(coeffs[:, max(0, distance * clusters - 6) :])
            right_parts[distance].append(coeffs[:, : min(clusters, 6 - (distance - 1) * clusters)])
    from_left = [None, None, None, None]
    from_right = [None, None, None, None]
    halo_size = rows * width
    for distance in range(1, 4):
        packed_left = jnp.concatenate(left_parts[distance], axis=1)
        packed_right = jnp.concatenate(right_parts[distance], axis=1)
        if distance == 1:
            flat_left = jnp.concatenate(
                [stacked[:, -width:].reshape(-1), packed_left.reshape(-1)]
            )
            flat_right = jnp.concatenate(
                [stacked[:, :width].reshape(-1), packed_right.reshape(-1)]
            )
            got_left = exchange(flat_left, 1)
            got_right = exchange(flat_right, -1)
            halo_before = got_left[:halo_size].reshape(rows, width)
            halo_after = got_right[:halo_size].reshape(rows, width)
            from_left[1] = got_left[halo_size:].reshape(packed_left.shape)
            from_right[1] = got_right[halo_size:].reshape(packed_right.shape)
        else:
            from_left[distance] = exchange(packed_left, distance)
            from_right[distance] = exchange(packed_right, -distance)
    widened = jnp.concatenate([halo_before, stacked, halo_after], axis=1)
    near_part = near_field(widened[:right_sides], widened[right_sides:], near_mask)
    cursors_left = [0, 0, 0, 0]
    cursors_right = [0, 0, 0, 0]
    coupled_local = []
    for tree_level in range(LOG_LD):
        coeffs = upward[tree_level]
        clusters = coeffs.shape[1]
        reach_devices = -(-6 // clusters)
        before = []
        beyond = []
        for distance in range(reach_devices, 0, -1):
            piece_width = clusters - max(0, distance * clusters - 6)
            before.append(
                from_left[distance][
                    :, cursors_left[distance] : cursors_left[distance] + piece_width
                ]
            )
            cursors_left[distance] += piece_width
        for distance in range(1, reach_devices + 1):
            piece_width = min(clusters, 6 - (distance - 1) * clusters)
            beyond.append(
                from_right[distance][
                    :, cursors_right[distance] : cursors_right[distance] + piece_width
                ]
            )
            cursors_right[distance] += piece_width
        padded = jnp.concatenate(before + [coeffs] + beyond, axis=1)
        first_row = 2 * LEAF_DEV - 2 * clusters
        live_slots = lower_mask[0][:, first_row : first_row + clusters].astype(jnp.float32)
        is_even = (jnp.arange(clusters) % 2 == 0).astype(jnp.float32)
        coupled_local.append(
            couple_window(padded, coupling[tree_level], slot_weights(live_slots, is_even), 6)
        )
    far_field = upper_far_field(
        upward[LOG_LD][:, 0], device_index, device_count, upper_mask, transfer, coupling
    )
    far_field = far_field[:, None, :]
    for tree_level in range(LOG_LD - 1, -1, -1):
        far_field = coupled_local[tree_level] + lower_pairs(transfer[tree_level], far_field)
    far_part = jnp.einsum("klr,kla->rla", far_field, leaf_basis, precision=highest).reshape(
        right_sides, LEAF_DEV * LS
    )
    potential_tree = near_part + far_part
    return jnp.zeros_like(potential_tree).at[:, tree_positions].set(potential_tree)


def solution(mesh):
    placed = (
        P(None, ("group", "leaf")),
        P(None, ("group", "leaf")),
        P(("group", "leaf"), None),
        P(None, ("group", "leaf")),
        P(None, ("group", "leaf")),
        P(("group", "leaf"), None, None),
        P(),
        P(),
        P(),
    )
    return jax.shard_map(
        local, mesh=mesh, in_specs=placed, out_specs=P(None, ("group", "leaf")), check_vma=False
    )
```

```python
import jax
import jax.numpy as jnp
from jax import lax
from jax.sharding import PartitionSpec as P
from jax.experimental import pallas as pl
from jax.experimental.pallas import tpu as pltpu

K = 64
LS = 64
LEAF_DEV = 32
LOG_LD = 5


KERNEL_SCALE = 0.0625
SOFTENING = 0.01
OFFSETS = (-7, -6, -5, -4, 4, 5, 6, 7)
highest = lax.Precision.HIGH


def from_behind(shard, axis, by):
    peers = lax.axis_size(axis)
    pairs = [(i, i + by) for i in range(peers) if 0 <= i + by < peers]
    return lax.ppermute(shard, axis, pairs)


def extended_2(shard, sides, width):
    for axis, dim in sides:
        peers, length = (lax.axis_size(axis), shard.shape[dim])
        up = [(i, (i + 1) % peers) for i in range(peers - 1)]
        down = [(j, i) for i, j in up]
        last = lax.slice_in_dim(shard, length - width, length, axis=dim)
        first = lax.slice_in_dim(shard, 0, width, axis=dim)
        before = lax.ppermute(last, axis, up)
        after = lax.ppermute(first, axis, down)
        shard = jnp.concatenate([before, shard, after], axis=dim)
    return shard


def from_partner(block, axis, stride):
    count = lax.axis_size(axis)
    route = []
    for low in range(count):
        high = low | 1 << stride
        if high != low and high < count:
            route += [(low, high), (high, low)]
    return lax.ppermute(block, axis, route)


NEAR_REACH = 3


def near_kernel(charge_ref, point_ref, column_ref, weight_ref, out_ref):
    leaves = weight_ref.shape[0]
    span = (2 * NEAR_REACH + 1) * LS
    blocks = []
    for leaf in range(leaves):
        first = leaf * LS
        source = column_ref[first : first + span, :]
        squared = None
        for axis in range(3):
            target = point_ref[axis : axis + 1, first + NEAR_REACH * LS : first + (NEAR_REACH + 1) * LS]
            gap = source[:, axis : axis + 1] - target
            squared = gap * gap if squared is None else squared + gap * gap
        kernel = KERNEL_SCALE * lax.rsqrt(squared + SOFTENING)
        charges = charge_ref[:, first : first + span] * weight_ref[leaf : leaf + 1, :]
        blocks.append(
            jnp.dot(
                charges, kernel, precision=lax.Precision.HIGHEST, preferred_element_type=jnp.float32
            )
        )
    out_ref[...] = jnp.concatenate(blocks, axis=1)


def near_field(charge_window, point_window, near_mask):
    leaves = near_mask.shape[1]
    right_sides = charge_window.shape[0]
    masks = near_mask.astype(jnp.float32)
    ones = jnp.ones((1, leaves), jnp.float32)
    weight = jnp.concatenate([masks[:NEAR_REACH], ones, masks[NEAR_REACH:]], axis=0).T
    weight = jnp.repeat(weight, LS, axis=1)
    whole = pl.BlockSpec(memory_space=pltpu.VMEM)
    return pl.pallas_call(
        near_kernel,
        out_shape=jax.ShapeDtypeStruct((right_sides, leaves * LS), jnp.float32),
        in_specs=[whole] * 4,
        out_specs=whole,
        cost_estimate=pl.CostEstimate(
            flops=2 * right_sides * leaves * LS * (2 * NEAR_REACH + 1) * LS * 6,
            transcendentals=leaves * LS * (2 * NEAR_REACH + 1) * LS,
            bytes_accessed=4 * (right_sides + 6) * (leaves + 6) * LS + 4 * right_sides * leaves * LS,
        ),
    )(charge_window, point_window, point_window.T, weight)


def slot_weights(live_slots, is_even):
    is_odd = 1.0 - is_even
    return (
        live_slots[6] * is_odd,
        live_slots[0],
        live_slots[1],
        live_slots[2],
        live_slots[3],
        live_slots[4],
        live_slots[5],
        live_slots[6] * is_even,
    )


def couple_window(padded, coupling_table, weights, reach_cells):
    clusters = padded.shape[1] - 2 * reach_cells
    extended = jnp.pad(padded, ((0, 0), (1, 1), (0, 0)))
    products = jnp.einsum("pij,jmr->pimr", coupling_table, extended, precision=highest)
    summed = None
    for position, offset in enumerate(OFFSETS):
        first_col = reach_cells + 1 + offset
        term = products[position, :, first_col : first_col + clusters] * weights[position][None, :, None]
        summed = term if summed is None else summed + term
    return summed


def raise_pairs(table, coeffs):
    pairs = coeffs.reshape(coeffs.shape[0], coeffs.shape[1] // 2, 2, coeffs.shape[2])
    return jnp.einsum("pjk,jcpr->kcr", table, pairs, precision=highest)


def lower_pairs(table, coeffs):
    children = jnp.einsum("pkj,jnr->knpr", table, coeffs, precision=highest)
    return children.reshape(coeffs.shape[0], 2 * coeffs.shape[1], coeffs.shape[2])


def raise_level(matrix, coeffs):
    return jnp.einsum("jk,jnr->knr", matrix, coeffs, precision=highest)


def lower_level(matrix, coeffs):
    return jnp.einsum("kj,jnr->knr", matrix, coeffs, precision=highest)


def alternate_children(first_child, second_child):
    stacked = jnp.stack([first_child, second_child], axis=2)
    return stacked.reshape(first_child.shape[0], 2 * first_child.shape[1], first_child.shape[2])


AXES = ("group", "leaf")


def exchange(shard, by):
    return from_behind(shard, AXES, by)


def upper_far_field(top, device_index, device_count, upper_mask, transfer, coupling):
    log_dev = device_count.bit_length() - 1
    levels = [lax.all_gather(top.T, AXES, axis=0, tiled=False)]
    for height in range(log_dev - 4):
        coeffs = levels[-1]
        pairs = coeffs.reshape(coeffs.shape[0] // 2, 2, coeffs.shape[1], coeffs.shape[2])
        levels.append(
            jnp.einsum("cprj,pjk->crk", pairs, transfer[LOG_LD + height], precision=highest)
        )
    reach = max(OFFSETS)
    picks = [reach + offset for offset in OFFSETS]
    windows = []
    for height in range(log_dev - 3):
        coeffs = levels[height]
        clusters = coeffs.shape[0]
        cluster = device_index // 2**height
        padded = jnp.pad(coeffs, ((reach, reach), (0, 0), (0, 0)))
        window = lax.dynamic_slice_in_dim(padded, cluster, 2 * reach + 1, axis=0)
        window = jnp.concatenate([window[: picks[3] + 1], window[picks[4] :]], axis=0)
        mask_row = 2 * device_count - 2 * clusters + cluster
        live_slots = lax.dynamic_index_in_dim(upper_mask, mask_row, 1, keepdims=False).astype(
            jnp.float32
        )
        weights = jnp.stack(slot_weights(live_slots, (cluster % 2 == 0).astype(jnp.float32)))
        windows.append(window * weights[:, None, None])
    stacked = jnp.stack(windows)
    coupled = jnp.einsum(
        "hpij,hprj->hri", coupling[LOG_LD : LOG_LD + log_dev - 3], stacked, precision=highest
    )
    far_field = coupled[-1]
    for height in range(log_dev - 5, -1, -1):
        side_bit = device_index // 2**height % 2
        far_field = coupled[height] + jnp.einsum(
            "rj,kj->rk", far_field, transfer[LOG_LD + height][side_bit], precision=highest
        )
    return far_field.T


def local(
    charge_input,
    points,
    tree_order,
    cluster_basis,
    near_mask,
    lower_mask,
    upper_mask,
    transfer,
    coupling,
):
    device_count = lax.axis_size(AXES)
    device_index = lax.axis_index(AXES)
    tree_positions = tree_order[0]
    right_sides = charge_input.shape[0]
    stacked = jnp.concatenate([charge_input, points], axis=0)[:, tree_positions]
    charges = stacked[:right_sides]
    rows, width = stacked.shape[0], 3 * LS
    leaf_basis = cluster_basis.reshape(K, LEAF_DEV, LS)
    upward = [
        jnp.einsum(
            "kla,rla->klr",
            leaf_basis,
            charges.reshape(right_sides, LEAF_DEV, LS),
            precision=highest,
        )
    ]
    for tree_level in range(LOG_LD):
        coeffs = upward[-1]
        upward.append(raise_pairs(transfer[tree_level], coeffs))
    left_parts = [[], [], [], []]
    right_parts = [[], [], [], []]
    for tree_level in range(LOG_LD):
        coeffs = upward[tree_level]
        clusters = coeffs.shape[1]
        for distance in range(1, -(-6 // clusters) + 1):
            left_parts[distance].append(coeffs[:, max(0, distance * clusters - 6) :])
            right_parts[distance].append(coeffs[:, : min(clusters, 6 - (distance - 1) * clusters)])
    from_left = [None, None, None, None]
    from_right = [None, None, None, None]
    halo_size = rows * width
    for distance in range(1, 4):
        packed_left = jnp.concatenate(left_parts[distance], axis=1)
        packed_right = jnp.concatenate(right_parts[distance], axis=1)
        if distance == 1:
            flat_left = jnp.concatenate(
                [stacked[:, -width:].reshape(-1), packed_left.reshape(-1)]
            )
            flat_right = jnp.concatenate(
                [stacked[:, :width].reshape(-1), packed_right.reshape(-1)]
            )
            got_left = exchange(flat_left, 1)
            got_right = exchange(flat_right, -1)
            halo_before = got_left[:halo_size].reshape(rows, width)
            halo_after = got_right[:halo_size].reshape(rows, width)
            from_left[1] = got_left[halo_size:].reshape(packed_left.shape)
            from_right[1] = got_right[halo_size:].reshape(packed_right.shape)
        else:
            from_left[distance] = exchange(packed_left, distance)
            from_right[distance] = exchange(packed_right, -distance)
    widened = jnp.concatenate([halo_before, stacked, halo_after], axis=1)
    near_part = near_field(widened[:right_sides], widened[right_sides:], near_mask)
    cursors_left = [0, 0, 0, 0]
    cursors_right = [0, 0, 0, 0]
    coupled_local = []
    for tree_level in range(LOG_LD):
        coeffs = upward[tree_level]
        clusters = coeffs.shape[1]
        reach_devices = -(-6 // clusters)
        before = []
        beyond = []
        for distance in range(reach_devices, 0, -1):
            piece_width = clusters - max(0, distance * clusters - 6)
            before.append(
                from_left[distance][
                    :, cursors_left[distance] : cursors_left[distance] + piece_width
                ]
            )
            cursors_left[distance] += piece_width
        for distance in range(1, reach_devices + 1):
            piece_width = min(clusters, 6 - (distance - 1) * clusters)
            beyond.append(
                from_right[distance][
                    :, cursors_right[distance] : cursors_right[distance] + piece_width
                ]
            )
            cursors_right[distance] += piece_width
        padded = jnp.concatenate(before + [coeffs] + beyond, axis=1)
        first_row = 2 * LEAF_DEV - 2 * clusters
        live_slots = lower_mask[0][:, first_row : first_row + clusters].astype(jnp.float32)
        is_even = (jnp.arange(clusters) % 2 == 0).astype(jnp.float32)
        coupled_local.append(
            couple_window(padded, coupling[tree_level], slot_weights(live_slots, is_even), 6)
        )
    far_field = upper_far_field(
        upward[LOG_LD][:, 0], device_index, device_count, upper_mask, transfer, coupling
    )
    far_field = far_field[:, None, :]
    for tree_level in range(LOG_LD - 1, -1, -1):
        far_field = coupled_local[tree_level] + lower_pairs(transfer[tree_level], far_field)
    far_part = jnp.einsum("klr,kla->rla", far_field, leaf_basis, precision=highest).reshape(
        right_sides, LEAF_DEV * LS
    )
    potential_tree = near_part + far_part
    return jnp.zeros_like(potential_tree).at[:, tree_positions].set(potential_tree)


def solution(mesh):
    placed = (
        P(None, ("group", "leaf")),
        P(None, ("group", "leaf")),
        P(("group", "leaf"), None),
        P(None, ("group", "leaf")),
        P(None, ("group", "leaf")),
        P(("group", "leaf"), None, None),
        P(),
        P(),
        P(),
    )
    return jax.shard_map(
        local, mesh=mesh, in_specs=placed, out_specs=P(None, ("group", "leaf")), check_vma=False
    )
```

```python
import jax
import jax.numpy as jnp
from jax import lax
from jax.sharding import PartitionSpec as P
from jax.experimental import pallas as pl
from jax.experimental.pallas import tpu as pltpu

K = 64
LS = 64
LEAF_DEV = 32
LOG_LD = 5


KERNEL_SCALE = 0.0625
SOFTENING = 0.01
OFFSETS = (-7, -6, -5, -4, 4, 5, 6, 7)
highest = lax.Precision.HIGH


def from_behind(shard, axis, by):
    peers = lax.axis_size(axis)
    pairs = [(i, i + by) for i in range(peers) if 0 <= i + by < peers]
    return lax.ppermute(shard, axis, pairs)


NEAR_REACH = 3


def near_kernel(charge_ref, point_ref, column_ref, weight_ref, out_ref):
    leaves = weight_ref.shape[0]
    span = (2 * NEAR_REACH + 1) * LS
    blocks = []
    for leaf in range(leaves):
        first = leaf * LS
        source = column_ref[first : first + span, :]
        squared = None
        for axis in range(3):
            target = point_ref[axis : axis + 1, first + NEAR_REACH * LS : first + (NEAR_REACH + 1) * LS]
            gap = source[:, axis : axis + 1] - target
            squared = gap * gap if squared is None else squared + gap * gap
        kernel = KERNEL_SCALE * lax.rsqrt(squared + SOFTENING)
        charges = charge_ref[:, first : first + span] * weight_ref[leaf : leaf + 1, :]
        blocks.append(
            jnp.dot(
                charges, kernel, precision=highest, preferred_element_type=jnp.float32
            )
        )
    out_ref[...] = jnp.concatenate(blocks, axis=1)


def near_field(charge_window, point_window, near_mask):
    leaves = near_mask.shape[1]
    right_sides = charge_window.shape[0]
    masks = near_mask.astype(jnp.float32)
    ones = jnp.ones((1, leaves), jnp.float32)
    weight = jnp.concatenate([masks[:NEAR_REACH], ones, masks[NEAR_REACH:]], axis=0).T
    weight = jnp.repeat(weight, LS, axis=1)
    whole = pl.BlockSpec(memory_space=pltpu.VMEM)
    return pl.pallas_call(
        near_kernel,
        out_shape=jax.ShapeDtypeStruct((right_sides, leaves * LS), jnp.float32),
        in_specs=[whole] * 4,
        out_specs=whole,
        cost_estimate=pl.CostEstimate(
            flops=2 * right_sides * leaves * LS * (2 * NEAR_REACH + 1) * LS * 6,
            transcendentals=leaves * LS * (2 * NEAR_REACH + 1) * LS,
            bytes_accessed=4 * (right_sides + 6) * (leaves + 6) * LS + 4 * right_sides * leaves * LS,
        ),
    )(charge_window, point_window, point_window.T, weight)


def slot_weights(live_slots, is_even):
    is_odd = 1.0 - is_even
    return (
        live_slots[6] * is_odd,
        live_slots[0],
        live_slots[1],
        live_slots[2],
        live_slots[3],
        live_slots[4],
        live_slots[5],
        live_slots[6] * is_even,
    )


def couple_window(padded, coupling_table, weights, reach_cells):
    clusters = padded.shape[1] - 2 * reach_cells
    extended = jnp.pad(padded, ((0, 0), (1, 1), (0, 0)))
    products = jnp.einsum("pij,jmr->pimr", coupling_table, extended, precision=highest)
    summed = None
    for position, offset in enumerate(OFFSETS):
        first_col = reach_cells + 1 + offset
        term = products[position, :, first_col : first_col + clusters] * weights[position][None, :, None]
        summed = term if summed is None else summed + term
    return summed


def raise_pairs(table, coeffs):
    pairs = coeffs.reshape(coeffs.shape[0], coeffs.shape[1] // 2, 2, coeffs.shape[2])
    return jnp.einsum("pjk,jcpr->kcr", table, pairs, precision=highest)


def lower_pairs(table, coeffs):
    children = jnp.einsum("pkj,jnr->knpr", table, coeffs, precision=highest)
    return children.reshape(coeffs.shape[0], 2 * coeffs.shape[1], coeffs.shape[2])


AXES = ("group", "leaf")


def exchange(shard, by):
    return from_behind(shard, AXES, by)


def upper_far_field(top, device_index, device_count, upper_mask, transfer, coupling):
    log_dev = device_count.bit_length() - 1
    levels = [lax.all_gather(top.T, AXES, axis=0, tiled=False)]
    for height in range(log_dev - 4):
        coeffs = levels[-1]
        pairs = coeffs.reshape(coeffs.shape[0] // 2, 2, coeffs.shape[1], coeffs.shape[2])
        levels.append(
            jnp.einsum("cprj,pjk->crk", pairs, transfer[LOG_LD + height], precision=highest)
        )
    reach = max(OFFSETS)
    picks = [reach + offset for offset in OFFSETS]
    windows = []
    for height in range(log_dev - 3):
        coeffs = levels[height]
        clusters = coeffs.shape[0]
        cluster = device_index // 2**height
        padded = jnp.pad(coeffs, ((reach, reach), (0, 0), (0, 0)))
        window = lax.dynamic_slice_in_dim(padded, cluster, 2 * reach + 1, axis=0)
        window = jnp.concatenate([window[: picks[3] + 1], window[picks[4] :]], axis=0)
        mask_row = 2 * device_count - 2 * clusters + cluster
        live_slots = lax.dynamic_index_in_dim(upper_mask, mask_row, 1, keepdims=False).astype(
            jnp.float32
        )
        weights = jnp.stack(slot_weights(live_slots, (cluster % 2 == 0).astype(jnp.float32)))
        windows.append(window * weights[:, None, None])
    stacked = jnp.stack(windows)
    coupled = jnp.einsum(
        "hpij,hprj->hri", coupling[LOG_LD : LOG_LD + log_dev - 3], stacked, precision=highest
    )
    far_field = coupled[-1]
    for height in range(log_dev - 5, -1, -1):
        side_bit = device_index // 2**height % 2
        far_field = coupled[height] + jnp.einsum(
            "rj,kj->rk", far_field, transfer[LOG_LD + height][side_bit], precision=highest
        )
    return far_field.T


def local(
    charge_input,
    points,
    tree_order,
    cluster_basis,
    near_mask,
    lower_mask,
    upper_mask,
    transfer,
    coupling,
):
    device_count = lax.axis_size(AXES)
    device_index = lax.axis_index(AXES)
    tree_positions = tree_order[0]
    right_sides = charge_input.shape[0]
    stacked = jnp.concatenate([charge_input, points], axis=0)[:, tree_positions]
    charges = stacked[:right_sides]
    rows, width = stacked.shape[0], 3 * LS
    leaf_basis = cluster_basis.reshape(K, LEAF_DEV, LS)
    upward = [
        jnp.einsum(
            "kla,rla->klr",
            leaf_basis,
            charges.reshape(right_sides, LEAF_DEV, LS),
            precision=highest,
        )
    ]
    for tree_level in range(LOG_LD):
        coeffs = upward[-1]
        upward.append(raise_pairs(transfer[tree_level], coeffs))
    left_parts = [[], [], [], []]
    right_parts = [[], [], [], []]
    for tree_level in range(LOG_LD):
        coeffs = upward[tree_level]
        clusters = coeffs.shape[1]
        for distance in range(1, -(-6 // clusters) + 1):
            left_parts[distance].append(coeffs[:, max(0, distance * clusters - 6) :])
            right_parts[distance].append(coeffs[:, : min(clusters, 6 - (distance - 1) * clusters)])
    from_left = [None, None, None, None]
    from_right = [None, None, None, None]
    halo_size = rows * width
    for distance in range(1, 4):
        packed_left = jnp.concatenate(left_parts[distance], axis=1)
        packed_right = jnp.concatenate(right_parts[distance], axis=1)
        if distance == 1:
            flat_left = jnp.concatenate(
                [stacked[:, -width:].reshape(-1), packed_left.reshape(-1)]
            )
            flat_right = jnp.concatenate(
                [stacked[:, :width].reshape(-1), packed_right.reshape(-1)]
            )
            got_left = exchange(flat_left, 1)
            got_right = exchange(flat_right, -1)
            halo_before = got_left[:halo_size].reshape(rows, width)
            halo_after = got_right[:halo_size].reshape(rows, width)
            from_left[1] = got_left[halo_size:].reshape(packed_left.shape)
            from_right[1] = got_right[halo_size:].reshape(packed_right.shape)
        else:
            from_left[distance] = exchange(packed_left, distance)
            from_right[distance] = exchange(packed_right, -distance)
    widened = jnp.concatenate([halo_before, stacked, halo_after], axis=1)
    near_part = near_field(widened[:right_sides], widened[right_sides:], near_mask)
    cursors_left = [0, 0, 0, 0]
    cursors_right = [0, 0, 0, 0]
    coupled_local = []
    for tree_level in range(LOG_LD):
        coeffs = upward[tree_level]
        clusters = coeffs.shape[1]
        reach_devices = -(-6 // clusters)
        before = []
        beyond = []
        for distance in range(reach_devices, 0, -1):
            piece_width = clusters - max(0, distance * clusters - 6)
            before.append(
                from_left[distance][
                    :, cursors_left[distance] : cursors_left[distance] + piece_width
                ]
            )
            cursors_left[distance] += piece_width
        for distance in range(1, reach_devices + 1):
            piece_width = min(clusters, 6 - (distance - 1) * clusters)
            beyond.append(
                from_right[distance][
                    :, cursors_right[distance] : cursors_right[distance] + piece_width
                ]
            )
            cursors_right[distance] += piece_width
        padded = jnp.concatenate(before + [coeffs] + beyond, axis=1)
        first_row = 2 * LEAF_DEV - 2 * clusters
        live_slots = lower_mask[0][:, first_row : first_row + clusters].astype(jnp.float32)
        is_even = (jnp.arange(clusters) % 2 == 0).astype(jnp.float32)
        coupled_local.append(
            couple_window(padded, coupling[tree_level], slot_weights(live_slots, is_even), 6)
        )
    far_field = upper_far_field(
        upward[LOG_LD][:, 0], device_index, device_count, upper_mask, transfer, coupling
    )
    far_field = far_field[:, None, :]
    for tree_level in range(LOG_LD - 1, -1, -1):
        far_field = coupled_local[tree_level] + lower_pairs(transfer[tree_level], far_field)
    far_part = jnp.einsum("klr,kla->rla", far_field, leaf_basis, precision=highest).reshape(
        right_sides, LEAF_DEV * LS
    )
    potential_tree = near_part + far_part
    return jnp.zeros_like(potential_tree).at[:, tree_positions].set(potential_tree)


def solution(mesh):
    placed = (
        P(None, ("group", "leaf")),
        P(None, ("group", "leaf")),
        P(("group", "leaf"), None),
        P(None, ("group", "leaf")),
        P(None, ("group", "leaf")),
        P(("group", "leaf"), None, None),
        P(),
        P(),
        P(),
    )
    return jax.shard_map(
        local, mesh=mesh, in_specs=placed, out_specs=P(None, ("group", "leaf")), check_vma=False
    )
```
